128 devices in a mesh: section: 4 (over x), sample: 8 (over z, y_lo), tensor: 4 (over y_hi, core).
Axes of the slice: x: 4, y: 4 (y_hi: 2, y_lo: 2; y = y_hi * 2 + y_lo), z: 4, core: 2. Of those that a mesh axis runs over, the one named last changes fastest.
Arguments:
- queries: bfloat16 [4, 1024, 8192], P('section', 'sample', 'tensor'), may hold values from -4.5 to 4.5
- suffix_keys: bfloat16 [4, 1024, 1024], P('section', 'sample', 'tensor'), may hold values from -4.5 to 4.5
- suffix_values: bfloat16 [4, 1024, 1024], P('section', 'sample', 'tensor'), may hold values from -4.5 to 4.5
- output_grad: bfloat16 [4, 1024, 8192], P('section', 'sample', 'tensor'), may hold values from -192 to 192
- prefix_keys: bfloat16 [4, 4096, 1024], P('section', ('sample', 'tensor')), may hold values from -4.5 to 4.5
- prefix_values: bfloat16 [4, 4096, 1024], P('section', ('sample', 'tensor')), may hold values from -4.5 to 4.5
- kv_weight: bfloat16 [4, 8192, 2, 1024], P('section', None, None, 'tensor'), may hold values from -0.0625 to 0.0625
- prefix_states: bfloat16 [4, 4096, 8192], P('section', ('sample', 'tensor')), may hold values from -6 to 6
- norm_gain: bfloat16 [4, 8192], P('section'), may hold values from 0.099609375 to 1.8984375
- segment_ids: int32 [8, 128], P('sample'), may hold values from 0 to 1, never falling along the last dimension, each value on 1 to 96 neighbouring positions
- segment_prompt: int32 [8, 2], P('sample'), may hold values from 0 to 2
- block_table: int32 [3, 16], replicated, may hold values from 0 to 31, as said below
Outputs:
- query_grad: bfloat16 [4, 1024, 8192], P('section', 'sample', 'tensor')
- rollout_key_gradient: bfloat16 [4, 1024, 1024], P('section', 'sample', 'tensor')
- suffix_value_grad: bfloat16 [4, 1024, 1024], P('section', 'sample', 'tensor')
- prefix_key_grad: float32 [4, 4096, 1024], P('section', ('sample', 'tensor'))
- prefix_value_grad: float32 [4, 4096, 1024], P('section', ('sample', 'tensor'))
- prefix_state_gradient: float32 [4, 4096, 8192], P('section', ('sample', 'tensor'))
The draws below stay inside these ranges and needn't reach their ends.
Inputs may be any that keep to these rules, and one draw needn't show every extreme that they name: `block_table`: each row lists 16 distinct pages; its first 8 entries are the same pages in every row, and every page of the pool appears in some row.
All inputs are finite; a program needn't handle non-finite values.
Results may differ from the reference program's by a relative error of at most 0.024.
Values may be sent and summed in bfloat16 or wider, within the bound.
No kernel may reach another device: no remote copies, remote signals or barrier semaphores. Data moves between devices by JAX's collectives and lax.ppermute only.
A program may use at most 192 MiB of HBM per device.

```python
import math
import jax
import jax.numpy as jnp
import numpy as np
from jax import lax

D = 8192
QH = 64
KEY_VALUE_HEADS = 8
HEAD_SIZE = 128
PAGE = 128
SEG_DEV = 2
NPROMPT = 3
TOK_DEV = 128
LAYERS = 4
HEAD_GROUPS = 4
ROW_BLOCKS = 8
ROLLOUT_TOKENS = 1024
NPAGES = 32
PREFIX_POOL_ROWS = 4096


def page_order(key):
    return jax.random.permutation(jax.random.fold_in(key, 11), NPAGES).astype(jnp.int32)


def draw_block_table(key, part):
    page_perm = page_order(key)
    shared = NPAGES // 4
    table_rows = []
    for prompt in range(NPROMPT):
        own_pages = page_perm[shared * (1 + prompt):shared * (2 + prompt)]
        table_rows.append(jnp.concatenate([page_perm[:shared], own_pages]))
    return jnp.stack(table_rows).astype(jnp.int32)


def draw_prefix_keys(key, part):
    base_key = jax.random.fold_in(key, 13)
    key_draw = jnp.clip(jax.random.normal(base_key, (LAYERS, PREFIX_POOL_ROWS, KEY_VALUE_HEADS * HEAD_SIZE), jnp.float32), -4.5, 4.5)
    return key_draw.astype(jnp.bfloat16)


def draw_queries(key, part):
    base_key = jax.random.fold_in(key, 14)
    query_draw = jnp.clip(jax.random.normal(base_key, (LAYERS, ROLLOUT_TOKENS, QH * HEAD_SIZE), jnp.float32), -4.5, 4.5)
    return query_draw.astype(jnp.bfloat16)


def touch_ends(result, own_key, least, largest):
    index_at = [jax.random.randint(jax.random.fold_in(own_key, axis), (), 0, length) for axis, length in enumerate(result.shape)]
    longest = result.shape.index(max(result.shape))
    next_to = index_at[:longest] + [(index_at[longest] + 1) % result.shape[longest]] + index_at[longest + 1:]
    return result.at[tuple(index_at)].set(least).at[tuple(next_to)].set(largest)


def shard_levels(key, extent, split, least, high):
    def one(dim, shards_of):
        heights = jax.random.uniform(jax.random.fold_in(jax.random.fold_in(key, 6), dim), (shards_of,), jnp.float32, least / len(split), high / len(split))
        return jnp.repeat(jnp.exp(heights), extent[dim] // shards_of).reshape((-1,) + (1,) * (len(extent) - dim - 1))

    gain = one(*split[0])
    for cut in split[1:]:
        gain = gain * one(*cut)
    return gain


def split_up(number_of, total, reach, slope):
    portions = [(1 << 20) // math.isqrt(standing ** slope) + 1 for standing in range(2, number_of + 1)]
    rest, holding = total - reach - (number_of - 1), [1] * (number_of - 1)
    while rest > 0:
        free = [i for i in range(number_of - 1) if holding[i] < reach]
        pool, left = sum([portions[i] for i in free]), rest
        for i in free:
            addition = min(reach - holding[i], max(1, left * portions[i] // pool), rest)
            holding[i] = holding[i] + addition
            rest = rest - addition
    return np.array([reach] + holding)


def uneven_parts(stream_key, number_of, total, limit, lean):
    if number_of == 2:
        one = jax.random.randint(stream_key, (), max(1, total - limit), min(limit, total - 1) + 1)
        return jnp.stack([one, total - one])
    sizes = jnp.asarray(split_up(number_of, total, limit, lean), jnp.int32)
    twos = (number_of - 1) // 2
    giver, receiver = sizes[1:1 + 2 * twos:2], sizes[2:2 + 2 * twos:2]
    slack = jnp.minimum(giver - 1, limit - receiver)
    shifted = jax.random.randint(jax.random.fold_in(stream_key, 1), (twos,), 0, 1 << 20) % (slack + 1)
    sizes = sizes.at[1:1 + 2 * twos:2].set(giver - shifted).at[2:2 + 2 * twos:2].set(receiver + shifted)
    return sizes[jax.random.permutation(jax.random.fold_in(stream_key, 2), number_of)]


def scatter_about(rng, dims, deviation, reach, shards=(), kind=jnp.bfloat16):
    loudness = shard_levels(rng, dims, shards, -0.22, 0.18) if shards else 1.0
    result = jax.random.normal(rng, dims, jnp.float32) * deviation * loudness
    return jnp.minimum(jnp.maximum(result, -reach), reach).astype(kind)


def setup_inputs(seed: int = 0) -> dict:
    keys = jax.random.split(jax.random.key(seed), 13)
    queries = draw_queries(jax.random.fold_in(keys[12], 71), 0)
    suffix_keys = scatter_about(keys[1], (LAYERS, ROLLOUT_TOKENS, KEY_VALUE_HEADS * HEAD_SIZE), 1.0, 4.5, ((0, 4), (1, 8), (2, 4)))
    suffix_values = scatter_about(keys[2], (LAYERS, ROLLOUT_TOKENS, KEY_VALUE_HEADS * HEAD_SIZE), 1.0, 4.5, ((0, 4), (1, 8), (2, 4)))
    output_grad = scatter_about(keys[3], (LAYERS, ROLLOUT_TOKENS, QH * HEAD_SIZE), 32.0, 192.0, ((0, 4), (1, 8), (2, 4)))
    prefix_keys = draw_prefix_keys(jax.random.fold_in(keys[12], 71), 0)
    prefix_values = scatter_about(keys[5], (LAYERS, PREFIX_POOL_ROWS, KEY_VALUE_HEADS * HEAD_SIZE), 1.0, 4.5, ((0, 4), (1, 32)))
    kv_weight = scatter_about(keys[6], (LAYERS, D, 2, KEY_VALUE_HEADS * HEAD_SIZE), D ** -0.5, 0.0625, ((0, 4), (3, 4)))
    prefix_states = scatter_about(keys[7], (LAYERS, PREFIX_POOL_ROWS, D), 1.0, 6.0, ((0, 4), (1, 32)))
    norm_gain = jnp.clip(1.0 + 0.18 * jax.random.normal(keys[8], (LAYERS, D), jnp.float32), 0.099609375, 1.8984375).astype(jnp.bfloat16)
    segment_ids = jax.vmap(lambda own: jnp.searchsorted(jnp.cumsum(uneven_parts(own, SEG_DEV, TOK_DEV, 3 * TOK_DEV // 4, 1)), jnp.arange(TOK_DEV), side="right"))(jax.random.split(keys[9], ROW_BLOCKS)).reshape((ROW_BLOCKS, TOK_DEV)).astype(jnp.int32)
    segment_prompt = touch_ends(jax.random.randint(keys[10], (ROW_BLOCKS, SEG_DEV), 0, NPROMPT), jax.random.fold_in(keys[10], 1), 0, NPROMPT - 1).astype(jnp.int32)
    block_table = draw_block_table(jax.random.fold_in(keys[12], 71), 0)
    return dict(queries=queries, suffix_keys=suffix_keys, suffix_values=suffix_values, output_grad=output_grad, prefix_keys=prefix_keys, prefix_values=prefix_values, kv_weight=kv_weight, prefix_states=prefix_states, norm_gain=norm_gain, segment_ids=segment_ids, segment_prompt=segment_prompt, block_table=block_table)


MASKED_SCORE = -1e+30
EPSILON = 1e-05

def visible_keys(seg_row, prompt_row, table, pooled_rows):
    tok_count = seg_row.shape[0]
    seg_hot = seg_row[:, None] == jnp.arange(prompt_row.shape[0], dtype=jnp.int32)[None, :]
    prompt_tok = lax.optimization_barrier(jnp.sum(jnp.where(seg_hot, prompt_row[None, :], 0), axis=1)).astype(jnp.int32)
    page_ids = jnp.arange(pooled_rows // PAGE, dtype=jnp.int32)
    member = jnp.any(table[:, :, None] == page_ids[None, None, :], axis=1)
    prompt_hot = prompt_tok[:, None] == jnp.arange(table.shape[0], dtype=jnp.int32)[None, :]
    member_tok = jnp.any(prompt_hot[:, :, None] & member[None, :, :], axis=1)
    prefix_seen = jnp.repeat(member_tok, PAGE, axis=1)
    position = jnp.arange(tok_count, dtype=jnp.int32)
    suffix_seen = (seg_row[:, None] == seg_row[None, :]) & (position[None, :] <= position[:, None])
    return jnp.concatenate([prefix_seen, suffix_seen], axis=1)

def attend_group(query_grp, grad_grp, key_rows, value_rows, visible):
    inv_root = query_grp.shape[-1] ** (-0.5)
    query_wide = query_grp.astype(jnp.float32)
    grad_wide = grad_grp.astype(jnp.float32)
    key_wide = key_rows.astype(jnp.float32)
    value_wide = value_rows.astype(jnp.float32)
    scores = jnp.einsum('rgd,kd->rgk', query_wide, key_wide) * inv_root
    scores = jnp.where(visible[:, None, :], scores, MASKED_SCORE)
    row_max = lax.optimization_barrier(jnp.max(scores, axis=2, keepdims=True))
    exponent = jnp.exp(scores - row_max)
    softmax_w = exponent / lax.optimization_barrier(jnp.sum(exponent, axis=2, keepdims=True))
    weights_low = softmax_w.astype(jnp.bfloat16).astype(jnp.float32)
    attended = jnp.einsum('rgk,kd->rgd', weights_low, value_wide)
    delta_row = lax.optimization_barrier(jnp.sum(grad_wide * attended, axis=2, keepdims=True))
    weight_grad = jnp.einsum('rgd,kd->rgk', grad_wide, value_wide)
    score_grad = (softmax_w * (weight_grad - delta_row)).astype(jnp.bfloat16).astype(jnp.float32)
    query_out = jnp.einsum('rgk,kd->rgd', score_grad, key_wide) * inv_root
    key_result = jnp.einsum('rgk,rgd->kd', score_grad, query_wide) * inv_root
    value_out = jnp.einsum('rgk,rgd->kd', weights_low, grad_wide)
    return (query_out, key_result, value_out)

def reference(queries, suffix_keys, suffix_values, output_grad, prefix_keys, prefix_values, kv_weight, prefix_states, norm_gain, segment_ids, segment_prompt, block_table):
    group_size = QH // KEY_VALUE_HEADS
    col_width = KEY_VALUE_HEADS * HEAD_SIZE // HEAD_GROUPS
    query_full, suffix_key_full, suffix_value_full, prefix_key_full, prefix_value_full, term_list = ([], [], [], [], [], [])
    for layer_idx in range(LAYERS):
        key_pool = prefix_keys[layer_idx]
        value_pool = prefix_values[layer_idx]

        def single_block(carry, block_args):
            query_b, grad_b, key_b, value_b, seg_row, prompt_row = block_args
            visible = visible_keys(seg_row, prompt_row, block_table, PREFIX_POOL_ROWS)
            query_h = query_b.reshape(TOK_DEV, KEY_VALUE_HEADS, group_size, HEAD_SIZE)
            grad_h = grad_b.reshape(TOK_DEV, KEY_VALUE_HEADS, group_size, HEAD_SIZE)
            query_pieces, suffix_key_pieces, suffix_value_pieces, prefix_key_pieces, prefix_value_pieces = ([], [], [], [], [])
            for head_index in range(KEY_VALUE_HEADS):
                col_range = slice(head_index * HEAD_SIZE, (head_index + 1) * HEAD_SIZE)
                key_rows = jnp.concatenate([key_pool[:, col_range], key_b[:, col_range]], axis=0)
                value_rows = jnp.concatenate([value_pool[:, col_range], value_b[:, col_range]], axis=0)
                query_out, key_result, value_out = attend_group(query_h[:, head_index], grad_h[:, head_index], key_rows, value_rows, visible)
                query_pieces.append(query_out)
                prefix_key_pieces.append(key_result[:PREFIX_POOL_ROWS])
                suffix_key_pieces.append(key_result[PREFIX_POOL_ROWS:])
                prefix_value_pieces.append(value_out[:PREFIX_POOL_ROWS])
                suffix_value_pieces.append(value_out[PREFIX_POOL_ROWS:])
            query_grad_block = jnp.stack(query_pieces, axis=1).reshape(TOK_DEV, QH * HEAD_SIZE).astype(jnp.bfloat16)
            suffix_key_block = jnp.concatenate(suffix_key_pieces, axis=1).astype(jnp.bfloat16)
            suffix_value_block = jnp.concatenate(suffix_value_pieces, axis=1).astype(jnp.bfloat16)
            next_carry = (carry[0] + jnp.concatenate(prefix_key_pieces, axis=1), carry[1] + jnp.concatenate(prefix_value_pieces, axis=1))
            return (next_carry, (query_grad_block, suffix_key_block, suffix_value_block))
        block_list = (queries[layer_idx].reshape(ROW_BLOCKS, TOK_DEV, QH * HEAD_SIZE), output_grad[layer_idx].reshape(ROW_BLOCKS, TOK_DEV, QH * HEAD_SIZE), suffix_keys[layer_idx].reshape(ROW_BLOCKS, TOK_DEV, KEY_VALUE_HEADS * HEAD_SIZE), suffix_values[layer_idx].reshape(ROW_BLOCKS, TOK_DEV, KEY_VALUE_HEADS * HEAD_SIZE), segment_ids, segment_prompt)
        empty_sums = (jnp.zeros((PREFIX_POOL_ROWS, KEY_VALUE_HEADS * HEAD_SIZE), jnp.float32), jnp.zeros((PREFIX_POOL_ROWS, KEY_VALUE_HEADS * HEAD_SIZE), jnp.float32))
        (pooled_key, pooled_value), (query_grad_layer, suffix_key_layer, suffix_value_layer) = lax.scan(single_block, empty_sums, block_list)
        query_full.append(query_grad_layer.reshape(ROLLOUT_TOKENS, QH * HEAD_SIZE))
        suffix_key_full.append(suffix_key_layer.reshape(ROLLOUT_TOKENS, KEY_VALUE_HEADS * HEAD_SIZE))
        suffix_value_full.append(suffix_value_layer.reshape(ROLLOUT_TOKENS, KEY_VALUE_HEADS * HEAD_SIZE))
        prefix_key_full.append(pooled_key)
        prefix_value_full.append(pooled_value)
        key_low = pooled_key.astype(jnp.bfloat16)
        value_low = pooled_value.astype(jnp.bfloat16)
        normed_grad = jnp.zeros((PREFIX_POOL_ROWS, D), jnp.float32)
        for group_idx in range(HEAD_GROUPS):
            col_range = slice(group_idx * col_width, (group_idx + 1) * col_width)
            grad_cols = jnp.concatenate([key_low[:, col_range], value_low[:, col_range]], axis=1)
            weight_cols = jnp.concatenate([kv_weight[layer_idx, :, 0, col_range], kv_weight[layer_idx, :, 1, col_range]], axis=1)
            group_term = lax.optimization_barrier(jnp.dot(grad_cols, weight_cols.T, preferred_element_type=jnp.float32).astype(jnp.bfloat16))
            normed_grad = normed_grad + group_term.astype(jnp.float32)
        states = prefix_states[layer_idx].astype(jnp.float32)
        gain_wide = norm_gain[layer_idx].astype(jnp.float32)[None, :]
        inv_rms = lax.rsqrt(lax.optimization_barrier(jnp.mean(states * states, axis=1, keepdims=True)) + EPSILON)
        gained = gain_wide * normed_grad
        layer_term = inv_rms * gained - states * inv_rms ** 3 * lax.optimization_barrier(jnp.mean(states * gained, axis=1, keepdims=True))
        term_list.append(layer_term)
    stacked_terms = jnp.stack(term_list, axis=0)
    prefix_state_gradient = jnp.flip(jnp.cumsum(jnp.flip(stacked_terms, 0), axis=0), 0)
    return (jnp.stack(query_full, 0), jnp.stack(suffix_key_full, 0), jnp.stack(suffix_value_full, 0), jnp.stack(prefix_key_full, 0), jnp.stack(prefix_value_full, 0), prefix_state_gradient)
```

```python
import jax
import jax.numpy as jnp
from jax import lax
from jax.sharding import PartitionSpec as P

HEAD_SIZE = 128
PAGE = 128


MASKED_SCORE = -1e30
EPSILON = 1e-05


def visible_keys(seg_row, prompt_row, table, pooled_rows):
    tok_count = seg_row.shape[0]
    seg_hot = seg_row[:, None] == jnp.arange(prompt_row.shape[0], dtype=jnp.int32)[None, :]
    prompt_tok = jnp.sum(jnp.where(seg_hot, prompt_row[None, :], 0), axis=1)
    page_ids = jnp.arange(pooled_rows // PAGE, dtype=jnp.int32)
    member = jnp.any(table[:, :, None] == page_ids[None, None, :], axis=1)
    prompt_hot = prompt_tok[:, None] == jnp.arange(table.shape[0], dtype=jnp.int32)[None, :]
    member_tok = jnp.any(prompt_hot[:, :, None] & member[None, :, :], axis=1)
    prefix_seen = jnp.repeat(member_tok, PAGE, axis=1)
    position = jnp.arange(tok_count, dtype=jnp.int32)
    suffix_seen = (seg_row[:, None] == seg_row[None, :]) & (position[None, :] <= position[:, None])
    return jnp.concatenate([prefix_seen, suffix_seen], axis=1)


def attend_group(query_grp, grad_grp, key_rows, value_rows, visible):
    inv_root = query_grp.shape[-1] ** (-0.5)
    scores = (
        jnp.einsum("rgd,kd->rgk", query_grp, key_rows, preferred_element_type=jnp.float32)
        * inv_root
    )
    scores = jnp.where(visible[:, None, :], scores, MASKED_SCORE)
    row_max = jnp.max(scores, axis=2, keepdims=True)
    exponent = jnp.exp(scores - row_max)
    softmax_w = exponent / jnp.sum(exponent, axis=2, keepdims=True)
    weights_low = softmax_w.astype(jnp.bfloat16)
    attended = jnp.einsum(
        "rgk,kd->rgd", weights_low, value_rows, preferred_element_type=jnp.float32
    )
    delta_row = jnp.sum(grad_grp.astype(jnp.float32) * attended, axis=2, keepdims=True)
    weight_grad = jnp.einsum(
        "rgd,kd->rgk", grad_grp, value_rows, preferred_element_type=jnp.float32
    )
    score_grad = (softmax_w * (weight_grad - delta_row)).astype(jnp.bfloat16)
    query_out = (
        jnp.einsum("rgk,kd->rgd", score_grad, key_rows, preferred_element_type=jnp.float32)
        * inv_root
    )
    key_result = (
        jnp.einsum("rgk,rgd->kd", score_grad, query_grp, preferred_element_type=jnp.float32)
        * inv_root
    )
    value_out = jnp.einsum("rgk,rgd->kd", weights_low, grad_grp, preferred_element_type=jnp.float32)
    return (query_out, key_result, value_out)


def make_body(n_sec, n_smp, n_ten):
    def on_device(
        queries,
        suffix_keys,
        suffix_values,
        output_grad,
        prefix_keys,
        prefix_values,
        kv_weight,
        prefix_states,
        norm_gain,
        segment_ids,
        segment_prompt,
        block_table,
    ):
        head_width = suffix_keys.shape[2]
        kv_local = head_width // HEAD_SIZE
        rows_local = prefix_keys.shape[1]
        pooled_rows = rows_local * n_smp * n_ten
        block_rows = rows_local * n_ten
        tok_count = queries.shape[1]
        group_size = queries.shape[2] // head_width
        visible = visible_keys(segment_ids[0], segment_prompt[0], block_table, pooled_rows)
        query_rows = queries[0].reshape(tok_count, kv_local, group_size, HEAD_SIZE)
        grad_rows = output_grad[0].reshape(tok_count, kv_local, group_size, HEAD_SIZE)
        own_keys = suffix_keys[0]
        own_values = suffix_values[0]
        pk = prefix_keys[0].reshape(rows_local, n_ten, kv_local, HEAD_SIZE)
        pv = prefix_values[0].reshape(rows_local, n_ten, kv_local, HEAD_SIZE)

        query_pieces, suffix_key_pieces, suffix_value_pieces, reduced_pieces = [], [], [], []
        for head_index in range(kv_local):
            low_col = head_index * HEAD_SIZE
            send = jnp.concatenate([pk[:, :, head_index], pv[:, :, head_index]], axis=-1)
            send = send.transpose(1, 0, 2)
            got = lax.all_to_all(send, "tensor", 0, 0, tiled=True)
            got = got.reshape(block_rows, 2 * HEAD_SIZE)
            pool = lax.all_gather(got, "sample", axis=0, tiled=True)
            key_rows = jnp.concatenate(
                [pool[:, :HEAD_SIZE], own_keys[:, low_col : low_col + HEAD_SIZE]], axis=0
            )
            value_rows = jnp.concatenate(
                [pool[:, HEAD_SIZE:], own_values[:, low_col : low_col + HEAD_SIZE]], axis=0
            )
            query_out, key_result, value_out = attend_group(
                query_rows[:, head_index], grad_rows[:, head_index], key_rows, value_rows, visible
            )
            query_pieces.append(query_out)
            suffix_key_pieces.append(key_result[pooled_rows:])
            suffix_value_pieces.append(value_out[pooled_rows:])
            pool_grad = jnp.concatenate(
                [key_result[:pooled_rows], value_out[:pooled_rows]], axis=1
            ).astype(jnp.bfloat16)
            reduced_pieces.append(
                lax.psum_scatter(pool_grad, "sample", scatter_dimension=0, tiled=True)
            )
        query_grad = jnp.stack(query_pieces, axis=1).reshape(tok_count, -1).astype(jnp.bfloat16)
        rollout_key_gradient = jnp.concatenate(suffix_key_pieces, axis=1).astype(jnp.bfloat16)
        suffix_value_grad = jnp.concatenate(suffix_value_pieces, axis=1).astype(jnp.bfloat16)

        reduced = jnp.concatenate(reduced_pieces, axis=1)
        home_send = reduced.reshape(n_ten, rows_local, kv_local * 2 * HEAD_SIZE)
        home = lax.all_to_all(home_send, "tensor", 0, 0, tiled=True)
        home = home.reshape(n_ten, rows_local, kv_local, 2, HEAD_SIZE).transpose(3, 1, 0, 2, 4)
        home = home.reshape(2, rows_local, n_ten * kv_local * HEAD_SIZE).astype(jnp.float32)
        key_home = home[0]
        value_home = home[1]

        grad_cols = reduced.reshape(block_rows, kv_local, 2, HEAD_SIZE).transpose(0, 2, 1, 3)
        grad_cols = grad_cols.reshape(block_rows, 2, kv_local * HEAD_SIZE)
        group_term = lax.dot_general(
            grad_cols, kv_weight[0], (((1, 2), (1, 2)), ((), ())), preferred_element_type=jnp.float32
        ).astype(jnp.bfloat16)
        width = group_term.shape[1]
        t_idx = lax.axis_index("tensor")
        core = t_idx % 2
        hi = t_idx // 2
        term4 = group_term.reshape(2, 2, rows_local, width)
        keep = lax.dynamic_index_in_dim(term4, core, 1, False)
        give = lax.dynamic_index_in_dim(term4, 1 - core, 1, False)
        core_pairs = [(i, i ^ 1) for i in range(n_ten)]
        got1 = lax.ppermute(give, "tensor", core_pairs)
        partial = keep.astype(jnp.float32) + got1.astype(jnp.float32)
        mine = lax.dynamic_index_in_dim(partial, hi, 0, False)
        other = lax.dynamic_index_in_dim(partial, 1 - hi, 0, False)
        chip_pairs = [(i, i ^ 2) for i in range(n_ten)]
        got2 = lax.ppermute(other.astype(jnp.bfloat16), "tensor", chip_pairs)
        normed_grad = mine + got2.astype(jnp.float32)

        states = prefix_states[0].astype(jnp.float32)
        gain_wide = norm_gain[0].astype(jnp.float32)[None, :]
        inv_rms = lax.rsqrt(jnp.mean(states * states, axis=1, keepdims=True) + EPSILON)
        gained = gain_wide * normed_grad
        layer_term = inv_rms * gained - states * inv_rms**3 * jnp.mean(
            states * gained, axis=1, keepdims=True
        )
        term_low = layer_term.astype(jnp.bfloat16)
        prefix_state_gradient = layer_term
        for shift in range(1, n_sec):
            pairs = [(l + shift, l) for l in range(n_sec - shift)]
            prefix_state_gradient = prefix_state_gradient + lax.ppermute(
                term_low, "section", pairs
            ).astype(jnp.float32)
        return (
            query_grad[None],
            rollout_key_gradient[None],
            suffix_value_grad[None],
            key_home[None],
            value_home[None],
            prefix_state_gradient[None],
        )

    return on_device


def solution(mesh):
    placed = (
        P("section", "sample", "tensor"),
        P("section", "sample", "tensor"),
        P("section", "sample", "tensor"),
        P("section", "sample", "tensor"),
        P("section", ("sample", "tensor"), None),
        P("section", ("sample", "tensor"), None),
        P("section", None, None, "tensor"),
        P("section", ("sample", "tensor"), None),
        P("section", None),
        P("sample", None),
        P("sample", None),
        P(),
    )
    body = make_body(mesh.shape["section"], mesh.shape["sample"], mesh.shape["tensor"])
    return jax.shard_map(
        body,
        mesh=mesh,
        in_specs=placed,
        out_specs=(
            P("section", "sample", "tensor"),
            P("section", "sample", "tensor"),
            P("section", "sample", "tensor"),
            P("section", ("sample", "tensor"), None),
            P("section", ("sample", "tensor"), None),
            P("section", ("sample", "tensor"), None),
        ),
        check_vma=False,
    )
```

```python
import jax
import jax.numpy as jnp
from jax import lax
from jax.sharding import PartitionSpec as P

HEAD_SIZE = 128
PAGE = 128


MASKED_SCORE = -1e30
EPSILON = 1e-05


def visible_keys(seg_row, prompt_row, table, pooled_rows):
    tok_count = seg_row.shape[0]
    seg_hot = seg_row[:, None] == jnp.arange(prompt_row.shape[0], dtype=jnp.int32)[None, :]
    prompt_tok = jnp.sum(jnp.where(seg_hot, prompt_row[None, :], 0), axis=1)
    page_ids = jnp.arange(pooled_rows // PAGE, dtype=jnp.int32)
    member = jnp.any(table[:, :, None] == page_ids[None, None, :], axis=1)
    prompt_hot = prompt_tok[:, None] == jnp.arange(table.shape[0], dtype=jnp.int32)[None, :]
    member_tok = jnp.any(prompt_hot[:, :, None] & member[None, :, :], axis=1)
    prefix_seen = jnp.repeat(member_tok, PAGE, axis=1)
    position = jnp.arange(tok_count, dtype=jnp.int32)
    suffix_seen = (seg_row[:, None] == seg_row[None, :]) & (position[None, :] <= position[:, None])
    return jnp.concatenate([prefix_seen, suffix_seen], axis=1)


def attend_group(query_grp, grad_grp, key_rows, value_rows, visible):
    inv_root = query_grp.shape[-1] ** (-0.5)
    scores = (
        jnp.einsum("rgd,kd->rgk", query_grp, key_rows, preferred_element_type=jnp.float32)
        * inv_root
    )
    scores = jnp.where(visible[:, None, :], scores, MASKED_SCORE)
    row_max = jnp.max(scores, axis=2, keepdims=True)
    exponent = jnp.exp(scores - row_max)
    softmax_w = exponent / jnp.sum(exponent, axis=2, keepdims=True)
    weights_low = softmax_w.astype(jnp.bfloat16)
    attended = jnp.einsum(
        "rgk,kd->rgd", weights_low, value_rows, preferred_element_type=jnp.float32
    )
    delta_row = jnp.sum(grad_grp.astype(jnp.float32) * attended, axis=2, keepdims=True)
    weight_grad = jnp.einsum(
        "rgd,kd->rgk", grad_grp, value_rows, preferred_element_type=jnp.float32
    )
    score_grad = (softmax_w * (weight_grad - delta_row)).astype(jnp.bfloat16)
    query_out = (
        jnp.einsum("rgk,kd->rgd", score_grad, key_rows, preferred_element_type=jnp.float32)
        * inv_root
    )
    key_result = (
        jnp.einsum("rgk,rgd->kd", score_grad, query_grp, preferred_element_type=jnp.float32)
        * inv_root
    )
    value_out = jnp.einsum("rgk,rgd->kd", weights_low, grad_grp, preferred_element_type=jnp.float32)
    return (query_out, key_result, value_out)


def make_body(n_sec, n_smp, n_ten):
    def on_device(
        queries,
        suffix_keys,
        suffix_values,
        output_grad,
        prefix_keys,
        prefix_values,
        kv_weight,
        prefix_states,
        norm_gain,
        segment_ids,
        segment_prompt,
        block_table,
    ):
        head_width = suffix_keys.shape[2]
        kv_local = head_width // HEAD_SIZE
        rows_local = prefix_keys.shape[1]
        pooled_rows = rows_local * n_smp * n_ten
        block_rows = rows_local * n_ten
        tok_count = queries.shape[1]
        group_size = queries.shape[2] // head_width
        visible = visible_keys(segment_ids[0], segment_prompt[0], block_table, pooled_rows)
        query_rows = queries[0].reshape(tok_count, kv_local, group_size, HEAD_SIZE)
        grad_rows = output_grad[0].reshape(tok_count, kv_local, group_size, HEAD_SIZE)
        own_keys = suffix_keys[0]
        own_values = suffix_values[0]
        pk = prefix_keys[0].reshape(rows_local, n_ten, kv_local, HEAD_SIZE)
        pv = prefix_values[0].reshape(rows_local, n_ten, kv_local, HEAD_SIZE)

        query_pieces, suffix_key_pieces, suffix_value_pieces, reduced_pieces = [], [], [], []
        for head_index in range(kv_local):
            low_col = head_index * HEAD_SIZE
            send = jnp.concatenate([pk[:, :, head_index], pv[:, :, head_index]], axis=-1)
            send = send.transpose(1, 0, 2)
            got = lax.all_to_all(send, "tensor", 0, 0, tiled=True)
            got = got.reshape(block_rows, 2 * HEAD_SIZE)
            spread = jnp.broadcast_to(got[None], (n_smp,) + got.shape)
            pool = lax.all_to_all(spread, "sample", 0, 0, tiled=True).reshape(pooled_rows, -1)
            key_rows = jnp.concatenate(
                [pool[:, :HEAD_SIZE], own_keys[:, low_col : low_col + HEAD_SIZE]], axis=0
            )
            value_rows = jnp.concatenate(
                [pool[:, HEAD_SIZE:], own_values[:, low_col : low_col + HEAD_SIZE]], axis=0
            )
            query_out, key_result, value_out = attend_group(
                query_rows[:, head_index], grad_rows[:, head_index], key_rows, value_rows, visible
            )
            query_pieces.append(query_out)
            suffix_key_pieces.append(key_result[pooled_rows:])
            suffix_value_pieces.append(value_out[pooled_rows:])
            pool_grad = jnp.concatenate(
                [key_result[:pooled_rows], value_out[:pooled_rows]], axis=1
            ).astype(jnp.bfloat16)
            pool_grad = pool_grad.reshape(n_smp, block_rows, 2 * HEAD_SIZE)
            parts = lax.all_to_all(pool_grad, "sample", 0, 0, tiled=False)
            reduced_pieces.append(jnp.sum(parts.astype(jnp.float32), axis=0))
        query_grad = jnp.stack(query_pieces, axis=1).reshape(tok_count, -1).astype(jnp.bfloat16)
        rollout_key_gradient = jnp.concatenate(suffix_key_pieces, axis=1).astype(jnp.bfloat16)
        suffix_value_grad = jnp.concatenate(suffix_value_pieces, axis=1).astype(jnp.bfloat16)

        reduced = jnp.concatenate(reduced_pieces, axis=1).astype(jnp.bfloat16)
        home_send = reduced.reshape(n_ten, rows_local, kv_local * 2 * HEAD_SIZE)
        home = lax.all_to_all(home_send, "tensor", 0, 0, tiled=True)
        home = home.reshape(n_ten, rows_local, kv_local, 2, HEAD_SIZE).transpose(3, 1, 0, 2, 4)
        home = home.reshape(2, rows_local, n_ten * kv_local * HEAD_SIZE).astype(jnp.float32)
        key_home = home[0]
        value_home = home[1]

        grad_cols = reduced.reshape(block_rows, kv_local, 2, HEAD_SIZE).transpose(0, 2, 1, 3)
        grad_cols = grad_cols.reshape(block_rows, 2, kv_local * HEAD_SIZE)
        group_term = lax.dot_general(
            grad_cols, kv_weight[0], (((1, 2), (1, 2)), ((), ())), preferred_element_type=jnp.float32
        ).astype(jnp.bfloat16)
        width = group_term.shape[1]
        t_idx = lax.axis_index("tensor")
        core = t_idx % 2
        hi = t_idx // 2
        term4 = group_term.reshape(2, 2, rows_local, width)
        keep = lax.dynamic_index_in_dim(term4, core, 1, False)
        give = lax.dynamic_index_in_dim(term4, 1 - core, 1, False)
        core_pairs = [(i, i ^ 1) for i in range(n_ten)]
        got1 = lax.ppermute(give, "tensor", core_pairs)
        partial = keep.astype(jnp.float32) + got1.astype(jnp.float32)
        mine = lax.dynamic_index_in_dim(partial, hi, 0, False)
        other = lax.dynamic_index_in_dim(partial, 1 - hi, 0, False)
        chip_pairs = [(i, i ^ 2) for i in range(n_ten)]
        got2 = lax.ppermute(other.astype(jnp.bfloat16), "tensor", chip_pairs)
        normed_grad = mine + got2.astype(jnp.float32)

        states = prefix_states[0].astype(jnp.float32)
        gain_wide = norm_gain[0].astype(jnp.float32)[None, :]
        inv_rms = lax.rsqrt(jnp.mean(states * states, axis=1, keepdims=True) + EPSILON)
        gained = gain_wide * normed_grad
        layer_term = inv_rms * gained - states * inv_rms**3 * jnp.mean(
            states * gained, axis=1, keepdims=True
        )
        term_low = layer_term.astype(jnp.bfloat16)
        terms = lax.all_gather(term_low, "section")
        above = jnp.arange(n_sec) > lax.axis_index("section")
        prefix_state_gradient = layer_term + jnp.sum(
            jnp.where(above[:, None, None], terms.astype(jnp.float32), 0.0), axis=0
        )
        return (
            query_grad[None],
            rollout_key_gradient[None],
            suffix_value_grad[None],
            key_home[None],
            value_home[None],
            prefix_state_gradient[None],
        )

    return on_device


def solution(mesh):
    placed = (
        P("section", "sample", "tensor"),
        P("section", "sample", "tensor"),
        P("section", "sample", "tensor"),
        P("section", "sample", "tensor"),
        P("section", ("sample", "tensor"), None),
        P("section", ("sample", "tensor"), None),
        P("section", None, None, "tensor"),
        P("section", ("sample", "tensor"), None),
        P("section", None),
        P("sample", None),
        P("sample", None),
        P(),
    )
    body = make_body(mesh.shape["section"], mesh.shape["sample"], mesh.shape["tensor"])
    return jax.shard_map(
        body,
        mesh=mesh,
        in_specs=placed,
        out_specs=(
            P("section", "sample", "tensor"),
            P("section", "sample", "tensor"),
            P("section", "sample", "tensor"),
            P("section", ("sample", "tensor"), None),
            P("section", ("sample", "tensor"), None),
            P("section", ("sample", "tensor"), None),
        ),
        check_vma=False,
    )
```

```python
import jax
import jax.numpy as jnp
from jax import lax
from jax.sharding import PartitionSpec as P

HEAD_SIZE = 128
PAGE = 128


MASKED_SCORE = -1e30
EPSILON = 1e-05


def visible_keys(seg_row, prompt_row, table, pooled_rows):
    tok_count = seg_row.shape[0]
    seg_hot = seg_row[:, None] == jnp.arange(prompt_row.shape[0], dtype=jnp.int32)[None, :]
    prompt_tok = jnp.sum(jnp.where(seg_hot, prompt_row[None, :], 0), axis=1)
    page_ids = jnp.arange(pooled_rows // PAGE, dtype=jnp.int32)
    member = jnp.any(table[:, :, None] == page_ids[None, None, :], axis=1)
    prompt_hot = prompt_tok[:, None] == jnp.arange(table.shape[0], dtype=jnp.int32)[None, :]
    member_tok = jnp.any(prompt_hot[:, :, None] & member[None, :, :], axis=1)
    prefix_seen = jnp.repeat(member_tok, PAGE, axis=1)
    position = jnp.arange(tok_count, dtype=jnp.int32)
    suffix_seen = (seg_row[:, None] == seg_row[None, :]) & (position[None, :] <= position[:, None])
    return jnp.concatenate([prefix_seen, suffix_seen], axis=1)


def attend_group(query_grp, grad_grp, key_rows, value_rows, visible):
    inv_root = query_grp.shape[-1] ** (-0.5)
    scores = (
        jnp.einsum("rgd,kd->rgk", query_grp, key_rows, preferred_element_type=jnp.float32)
        * inv_root
    )
    scores = jnp.where(visible[:, None, :], scores, MASKED_SCORE)
    row_max = jnp.max(scores, axis=2, keepdims=True)
    exponent = jnp.exp(scores - row_max)
    softmax_w = exponent / jnp.sum(exponent, axis=2, keepdims=True)
    weights_low = softmax_w.astype(jnp.bfloat16)
    attended = jnp.einsum(
        "rgk,kd->rgd", weights_low, value_rows, preferred_element_type=jnp.float32
    )
    delta_row = jnp.sum(grad_grp.astype(jnp.float32) * attended, axis=2, keepdims=True)
    weight_grad = jnp.einsum(
        "rgd,kd->rgk", grad_grp, value_rows, preferred_element_type=jnp.float32
    )
    score_grad = (softmax_w * (weight_grad - delta_row)).astype(jnp.bfloat16)
    query_out = (
        jnp.einsum("rgk,kd->rgd", score_grad, key_rows, preferred_element_type=jnp.float32)
        * inv_root
    )
    key_result = (
        jnp.einsum("rgk,rgd->kd", score_grad, query_grp, preferred_element_type=jnp.float32)
        * inv_root
    )
    value_out = jnp.einsum("rgk,rgd->kd", weights_low, grad_grp, preferred_element_type=jnp.float32)
    return (query_out, key_result, value_out)


def make_body(n_sec, n_smp, n_ten):
    def on_device(
        queries,
        suffix_keys,
        suffix_values,
        output_grad,
        prefix_keys,
        prefix_values,
        kv_weight,
        prefix_states,
        norm_gain,
        segment_ids,
        segment_prompt,
        block_table,
    ):
        head_width = suffix_keys.shape[2]
        kv_local = head_width // HEAD_SIZE
        rows_local = prefix_keys.shape[1]
        pooled_rows = rows_local * n_smp * n_ten
        block_rows = rows_local * n_ten
        tok_count = queries.shape[1]
        group_size = queries.shape[2] // head_width
        visible = visible_keys(segment_ids[0], segment_prompt[0], block_table, pooled_rows)
        query_rows = queries[0].reshape(tok_count, kv_local, group_size, HEAD_SIZE)
        grad_rows = output_grad[0].reshape(tok_count, kv_local, group_size, HEAD_SIZE)
        own_keys = suffix_keys[0]
        own_values = suffix_values[0]
        pk = prefix_keys[0].reshape(rows_local, n_ten, kv_local, 1, HEAD_SIZE)
        pv = prefix_values[0].reshape(rows_local, n_ten, kv_local, 1, HEAD_SIZE)
        send = jnp.concatenate([pk, pv], axis=3).reshape(rows_local, n_ten, -1).transpose(1, 0, 2)
        spread = jnp.broadcast_to(send[None], (n_smp,) + send.shape)
        spread = spread.reshape((n_smp * n_ten,) + send.shape[1:])
        pool_all = lax.all_to_all(spread, ("sample", "tensor"), 0, 0, tiled=True)
        pool_all = pool_all.reshape(pooled_rows, kv_local, 2, HEAD_SIZE)

        query_pieces, suffix_key_pieces, suffix_value_pieces, reduced_pieces = [], [], [], []
        for head_index in range(kv_local):
            low_col = head_index * HEAD_SIZE
            pool = pool_all[:, head_index].reshape(pooled_rows, 2 * HEAD_SIZE)
            key_rows = jnp.concatenate(
                [pool[:, :HEAD_SIZE], own_keys[:, low_col : low_col + HEAD_SIZE]], axis=0
            )
            value_rows = jnp.concatenate(
                [pool[:, HEAD_SIZE:], own_values[:, low_col : low_col + HEAD_SIZE]], axis=0
            )
            query_out, key_result, value_out = attend_group(
                query_rows[:, head_index], grad_rows[:, head_index], key_rows, value_rows, visible
            )
            query_pieces.append(query_out)
            suffix_key_pieces.append(key_result[pooled_rows:])
            suffix_value_pieces.append(value_out[pooled_rows:])
            pool_grad = jnp.concatenate(
                [key_result[:pooled_rows], value_out[:pooled_rows]], axis=1
            ).astype(jnp.bfloat16)
            pool_grad = pool_grad.reshape(n_smp, block_rows, 2 * HEAD_SIZE)
            parts = lax.all_to_all(pool_grad, "sample", 0, 0, tiled=False)
            reduced_pieces.append(jnp.sum(parts.astype(jnp.float32), axis=0))
        query_grad = jnp.stack(query_pieces, axis=1).reshape(tok_count, -1).astype(jnp.bfloat16)
        rollout_key_gradient = jnp.concatenate(suffix_key_pieces, axis=1).astype(jnp.bfloat16)
        suffix_value_grad = jnp.concatenate(suffix_value_pieces, axis=1).astype(jnp.bfloat16)

        reduced = jnp.concatenate(reduced_pieces, axis=1).astype(jnp.bfloat16)
        home_send = reduced.reshape(n_ten, rows_local, kv_local * 2 * HEAD_SIZE)
        home = lax.all_to_all(home_send, "tensor", 0, 0, tiled=True)
        home = home.reshape(n_ten, rows_local, kv_local, 2, HEAD_SIZE).transpose(3, 1, 0, 2, 4)
        home = home.reshape(2, rows_local, n_ten * kv_local * HEAD_SIZE).astype(jnp.float32)
        key_home = home[0]
        value_home = home[1]

        grad_cols = reduced.reshape(block_rows, kv_local, 2, HEAD_SIZE).transpose(0, 2, 1, 3)
        grad_cols = grad_cols.reshape(block_rows, 2, kv_local * HEAD_SIZE)
        group_term = lax.dot_general(
            grad_cols, kv_weight[0], (((1, 2), (1, 2)), ((), ())), preferred_element_type=jnp.float32
        ).astype(jnp.bfloat16)
        key_home, value_home, group_term = lax.optimization_barrier((key_home, value_home, group_term))
        width = group_term.shape[1]
        t_idx = lax.axis_index("tensor")
        core = t_idx % 2
        hi = t_idx // 2
        term4 = group_term.reshape(2, 2, rows_local, width)
        keep = lax.dynamic_index_in_dim(term4, core, 1, False)
        give = lax.dynamic_index_in_dim(term4, 1 - core, 1, False)
        core_pairs = [(i, i ^ 1) for i in range(n_ten)]
        got1 = lax.ppermute(give, "tensor", core_pairs)
        partial = keep.astype(jnp.float32) + got1.astype(jnp.float32)
        mine = lax.dynamic_index_in_dim(partial, hi, 0, False)
        other = lax.dynamic_index_in_dim(partial, 1 - hi, 0, False)
        chip_pairs = [(i, i ^ 2) for i in range(n_ten)]
        got2 = lax.ppermute(other.astype(jnp.bfloat16), "tensor", chip_pairs)
        normed_grad = mine + got2.astype(jnp.float32)

        states = prefix_states[0].astype(jnp.float32)
        gain_wide = norm_gain[0].astype(jnp.float32)[None, :]
        inv_rms = lax.rsqrt(jnp.mean(states * states, axis=1, keepdims=True) + EPSILON)
        gained = gain_wide * normed_grad
        layer_term = inv_rms * gained - states * inv_rms**3 * jnp.mean(
            states * gained, axis=1, keepdims=True
        )
        term_low = layer_term.astype(jnp.bfloat16)
        terms = lax.all_gather(term_low, "section")
        above = jnp.arange(n_sec) > lax.axis_index("section")
        prefix_state_gradient = layer_term + jnp.sum(
            jnp.where(above[:, None, None], terms.astype(jnp.float32), 0.0), axis=0
        )
        return (
            query_grad[None],
            rollout_key_gradient[None],
            suffix_value_grad[None],
            key_home[None],
            value_home[None],
            prefix_state_gradient[None],
        )

    return on_device


def solution(mesh):
    placed = (
        P("section", "sample", "tensor"),
        P("section", "sample", "tensor"),
        P("section", "sample", "tensor"),
        P("section", "sample", "tensor"),
        P("section", ("sample", "tensor"), None),
        P("section", ("sample", "tensor"), None),
        P("section", None, None, "tensor"),
        P("section", ("sample", "tensor"), None),
        P("section", None),
        P("sample", None),
        P("sample", None),
        P(),
    )
    body = make_body(mesh.shape["section"], mesh.shape["sample"], mesh.shape["tensor"])
    return jax.shard_map(
        body,
        mesh=mesh,
        in_specs=placed,
        out_specs=(
            P("section", "sample", "tensor"),
            P("section", "sample", "tensor"),
            P("section", "sample", "tensor"),
            P("section", ("sample", "tensor"), None),
            P("section", ("sample", "tensor"), None),
            P("section", ("sample", "tensor"), None),
        ),
        check_vma=False,
    )
```

```python
import jax
import jax.numpy as jnp
from jax import lax
from jax.sharding import PartitionSpec as P

HEAD_SIZE = 128
PAGE = 128


MASKED_SCORE = -1e30
EPSILON = 1e-05


def visible_keys(seg_row, prompt_row, table, pooled_rows):
    tok_count = seg_row.shape[0]
    seg_hot = seg_row[:, None] == jnp.arange(prompt_row.shape[0], dtype=jnp.int32)[None, :]
    prompt_tok = jnp.sum(jnp.where(seg_hot, prompt_row[None, :], 0), axis=1)
    page_ids = jnp.arange(pooled_rows // PAGE, dtype=jnp.int32)
    member = jnp.any(table[:, :, None] == page_ids[None, None, :], axis=1)
    prompt_hot = prompt_tok[:, None] == jnp.arange(table.shape[0], dtype=jnp.int32)[None, :]
    member_tok = jnp.any(prompt_hot[:, :, None] & member[None, :, :], axis=1)
    prefix_seen = jnp.repeat(member_tok, PAGE, axis=1)
    position = jnp.arange(tok_count, dtype=jnp.int32)
    suffix_seen = (seg_row[:, None] == seg_row[None, :]) & (position[None, :] <= position[:, None])
    return jnp.concatenate([prefix_seen, suffix_seen], axis=1)


def attend_group(query_grp, grad_grp, key_rows, value_rows, visible):
    inv_root = query_grp.shape[-1] ** (-0.5)
    scores = (
        jnp.einsum("rgd,kd->rgk", query_grp, key_rows, preferred_element_type=jnp.float32)
        * inv_root
    )
    scores = jnp.where(visible[:, None, :], scores, MASKED_SCORE)
    row_max = jnp.max(scores, axis=2, keepdims=True)
    exponent = jnp.exp(scores - row_max)
    softmax_w = exponent / jnp.sum(exponent, axis=2, keepdims=True)
    weights_low = softmax_w.astype(jnp.bfloat16)
    attended = jnp.einsum(
        "rgk,kd->rgd", weights_low, value_rows, preferred_element_type=jnp.float32
    )
    delta_row = jnp.sum(grad_grp.astype(jnp.float32) * attended, axis=2, keepdims=True)
    weight_grad = jnp.einsum(
        "rgd,kd->rgk", grad_grp, value_rows, preferred_element_type=jnp.float32
    )
    score_grad = (softmax_w * (weight_grad - delta_row)).astype(jnp.bfloat16)
    query_out = (
        jnp.einsum("rgk,kd->rgd", score_grad, key_rows, preferred_element_type=jnp.float32)
        * inv_root
    )
    key_result = (
        jnp.einsum("rgk,rgd->kd", score_grad, query_grp, preferred_element_type=jnp.float32)
        * inv_root
    )
    value_out = jnp.einsum("rgk,rgd->kd", weights_low, grad_grp, preferred_element_type=jnp.float32)
    return (query_out, key_result, value_out)


def make_body(n_sec, n_smp, n_ten):
    def on_device(
        queries,
        suffix_keys,
        suffix_values,
        output_grad,
        prefix_keys,
        prefix_values,
        kv_weight,
        prefix_states,
        norm_gain,
        segment_ids,
        segment_prompt,
        block_table,
    ):
        head_width = suffix_keys.shape[2]
        kv_local = head_width // HEAD_SIZE
        rows_local = prefix_keys.shape[1]
        pooled_rows = rows_local * n_smp * n_ten
        block_rows = rows_local * n_ten
        tok_count = queries.shape[1]
        group_size = queries.shape[2] // head_width
        visible = visible_keys(segment_ids[0], segment_prompt[0], block_table, pooled_rows)
        query_rows = queries[0].reshape(tok_count, kv_local, group_size, HEAD_SIZE)
        grad_rows = output_grad[0].reshape(tok_count, kv_local, group_size, HEAD_SIZE)
        own_keys = suffix_keys[0]
        own_values = suffix_values[0]
        pk = prefix_keys[0].reshape(rows_local, n_ten, kv_local, 1, HEAD_SIZE)
        pv = prefix_values[0].reshape(rows_local, n_ten, kv_local, 1, HEAD_SIZE)
        send = jnp.concatenate([pk, pv], axis=3).reshape(rows_local, n_ten, -1).transpose(1, 0, 2)
        got_all = lax.all_to_all(send, "tensor", 0, 0, tiled=True)
        got_all = got_all.reshape(block_rows, kv_local, 2 * HEAD_SIZE)

        query_pieces, suffix_key_pieces, suffix_value_pieces, reduced_pieces = [], [], [], []
        for head_index in range(kv_local):
            low_col = head_index * HEAD_SIZE
            got = got_all[:, head_index]
            if head_index % 2 == 0:
                spread = jnp.broadcast_to(got[None], (n_smp,) + got.shape)
                pool = lax.all_to_all(spread, "sample", 0, 0, tiled=True).reshape(pooled_rows, -1)
            else:
                pool = lax.all_gather(got, "sample", axis=0, tiled=True)
            key_rows = jnp.concatenate(
                [pool[:, :HEAD_SIZE], own_keys[:, low_col : low_col + HEAD_SIZE]], axis=0
            )
            value_rows = jnp.concatenate(
                [pool[:, HEAD_SIZE:], own_values[:, low_col : low_col + HEAD_SIZE]], axis=0
            )
            query_out, key_result, value_out = attend_group(
                query_rows[:, head_index], grad_rows[:, head_index], key_rows, value_rows, visible
            )
            query_pieces.append(query_out)
            suffix_key_pieces.append(key_result[pooled_rows:])
            suffix_value_pieces.append(value_out[pooled_rows:])
            pool_grad = jnp.concatenate(
                [key_result[:pooled_rows], value_out[:pooled_rows]], axis=1
            ).astype(jnp.bfloat16)
            pool_grad = pool_grad.reshape(n_smp, block_rows, 2 * HEAD_SIZE)
            parts = lax.all_to_all(pool_grad, "sample", 0, 0, tiled=False)
            reduced_pieces.append(jnp.sum(parts.astype(jnp.float32), axis=0))
        query_grad = jnp.stack(query_pieces, axis=1).reshape(tok_count, -1).astype(jnp.bfloat16)
        rollout_key_gradient = jnp.concatenate(suffix_key_pieces, axis=1).astype(jnp.bfloat16)
        suffix_value_grad = jnp.concatenate(suffix_value_pieces, axis=1).astype(jnp.bfloat16)

        reduced = jnp.concatenate(reduced_pieces, axis=1).astype(jnp.bfloat16)
        home_send = reduced.reshape(n_ten, rows_local, kv_local * 2 * HEAD_SIZE)
        home = lax.all_to_all(home_send, "tensor", 0, 0, tiled=True)
        home = home.reshape(n_ten, rows_local, kv_local, 2, HEAD_SIZE).transpose(3, 1, 0, 2, 4)
        home = home.reshape(2, rows_local, n_ten * kv_local * HEAD_SIZE).astype(jnp.float32)
        key_home = home[0]
        value_home = home[1]

        grad_cols = reduced.reshape(block_rows, kv_local, 2, HEAD_SIZE).transpose(0, 2, 1, 3)
        grad_cols = grad_cols.reshape(block_rows, 2, kv_local * HEAD_SIZE)
        group_term = lax.dot_general(
            grad_cols, kv_weight[0], (((1, 2), (1, 2)), ((), ())), preferred_element_type=jnp.float32
        ).astype(jnp.bfloat16)
        key_home, value_home, group_term = lax.optimization_barrier((key_home, value_home, group_term))
        width = group_term.shape[1]
        t_idx = lax.axis_index("tensor")
        core = t_idx % 2
        hi = t_idx // 2
        term4 = group_term.reshape(2, 2, rows_local, width)
        keep = lax.dynamic_index_in_dim(term4, core, 1, False)
        give = lax.dynamic_index_in_dim(term4, 1 - core, 1, False)
        core_pairs = [(i, i ^ 1) for i in range(n_ten)]
        chip_pairs = [(i, i ^ 2) for i in range(n_ten)]
        states_all = prefix_states[0]
        gain_wide = norm_gain[0].astype(jnp.float32)[None, :]
        sec = lax.axis_index("section")
        n_chunks = 2
        step = rows_local // n_chunks
        outs = []
        for c in range(n_chunks):
            rows = slice(c * step, (c + 1) * step)
            got1 = lax.ppermute(give[:, rows], "tensor", core_pairs)
            partial = keep[:, rows].astype(jnp.float32) + got1.astype(jnp.float32)
            mine = lax.dynamic_index_in_dim(partial, hi, 0, False)
            other = lax.dynamic_index_in_dim(partial, 1 - hi, 0, False)
            got2 = lax.ppermute(other.astype(jnp.bfloat16), "tensor", chip_pairs)
            normed_grad = mine + got2.astype(jnp.float32)

            states = states_all[rows].astype(jnp.float32)
            inv_rms = lax.rsqrt(jnp.mean(states * states, axis=1, keepdims=True) + EPSILON)
            gained = gain_wide * normed_grad
            layer_term = inv_rms * gained - states * inv_rms**3 * jnp.mean(
                states * gained, axis=1, keepdims=True
            )
            term_low = layer_term.astype(jnp.bfloat16)
            if n_sec == 4:
                down = lax.ppermute(term_low, "section", [(3, 2), (2, 1)])
                wrap = lax.ppermute(term_low, "section", [(3, 0)])
                carry = (
                    jnp.where(sec == 1, layer_term, 0.0)
                    + down.astype(jnp.float32)
                    + wrap.astype(jnp.float32)
                )
                last = lax.ppermute(carry.astype(jnp.bfloat16), "section", [(1, 0), (0, 1)])
                outs.append(
                    layer_term
                    + down.astype(jnp.float32)
                    + wrap.astype(jnp.float32)
                    + last.astype(jnp.float32)
                )
            else:
                terms = lax.all_gather(term_low, "section")
                above = jnp.arange(n_sec) > sec
                outs.append(
                    layer_term
                    + jnp.sum(jnp.where(above[:, None, None], terms.astype(jnp.float32), 0.0), axis=0)
                )
        prefix_state_gradient = jnp.concatenate(outs, axis=0)
        return (
            query_grad[None],
            rollout_key_gradient[None],
            suffix_value_grad[None],
            key_home[None],
            value_home[None],
            prefix_state_gradient[None],
        )

    return on_device


def solution(mesh):
    placed = (
        P("section", "sample", "tensor"),
        P("section", "sample", "tensor"),
        P("section", "sample", "tensor"),
        P("section", "sample", "tensor"),
        P("section", ("sample", "tensor"), None),
        P("section", ("sample", "tensor"), None),
        P("section", None, None, "tensor"),
        P("section", ("sample", "tensor"), None),
        P("section", None),
        P("sample", None),
        P("sample", None),
        P(),
    )
    body = make_body(mesh.shape["section"], mesh.shape["sample"], mesh.shape["tensor"])
    return jax.shard_map(
        body,
        mesh=mesh,
        in_specs=placed,
        out_specs=(
            P("section", "sample", "tensor"),
            P("section", "sample", "tensor"),
            P("section", "sample", "tensor"),
            P("section", ("sample", "tensor"), None),
            P("section", ("sample", "tensor"), None),
            P("section", ("sample", "tensor"), None),
        ),
        check_vma=False,
    )
```

```python
import jax
import jax.numpy as jnp
from jax import lax
from jax.sharding import PartitionSpec as P

HEAD_SIZE = 128
PAGE = 128


MASKED_SCORE = -1e30
EPSILON = 1e-05


def visible_keys(seg_row, prompt_row, table, pooled_rows):
    tok_count = seg_row.shape[0]
    seg_hot = seg_row[:, None] == jnp.arange(prompt_row.shape[0], dtype=jnp.int32)[None, :]
    prompt_tok = jnp.sum(jnp.where(seg_hot, prompt_row[None, :], 0), axis=1)
    page_ids = jnp.arange(pooled_rows // PAGE, dtype=jnp.int32)
    member = jnp.any(table[:, :, None] == page_ids[None, None, :], axis=1)
    prompt_hot = prompt_tok[:, None] == jnp.arange(table.shape[0], dtype=jnp.int32)[None, :]
    member_tok = jnp.any(prompt_hot[:, :, None] & member[None, :, :], axis=1)
    prefix_seen = jnp.repeat(member_tok, PAGE, axis=1)
    position = jnp.arange(tok_count, dtype=jnp.int32)
    suffix_seen = (seg_row[:, None] == seg_row[None, :]) & (position[None, :] <= position[:, None])
    return jnp.concatenate([prefix_seen, suffix_seen], axis=1)


def attend_group(query_grp, grad_grp, key_rows, value_rows, visible):
    inv_root = query_grp.shape[-1] ** (-0.5)
    scores = (
        jnp.einsum("rgd,kd->rgk", query_grp, key_rows, preferred_element_type=jnp.float32)
        * inv_root
    )
    scores = jnp.where(visible[:, None, :], scores, MASKED_SCORE)
    row_max = jnp.max(scores, axis=2, keepdims=True)
    exponent = jnp.exp(scores - row_max)
    softmax_w = exponent / jnp.sum(exponent, axis=2, keepdims=True)
    weights_low = softmax_w.astype(jnp.bfloat16)
    attended = jnp.einsum(
        "rgk,kd->rgd", weights_low, value_rows, preferred_element_type=jnp.float32
    )
    delta_row = jnp.sum(grad_grp.astype(jnp.float32) * attended, axis=2, keepdims=True)
    weight_grad = jnp.einsum(
        "rgd,kd->rgk", grad_grp, value_rows, preferred_element_type=jnp.float32
    )
    score_grad = (softmax_w * (weight_grad - delta_row)).astype(jnp.bfloat16)
    query_out = (
        jnp.einsum("rgk,kd->rgd", score_grad, key_rows, preferred_element_type=jnp.float32)
        * inv_root
    )
    key_result = (
        jnp.einsum("rgk,rgd->kd", score_grad, query_grp, preferred_element_type=jnp.float32)
        * inv_root
    )
    value_out = jnp.einsum("rgk,rgd->kd", weights_low, grad_grp, preferred_element_type=jnp.float32)
    return (query_out, key_result, value_out)


def make_body(n_sec, n_smp, n_ten):
    def on_device(
        queries,
        suffix_keys,
        suffix_values,
        output_grad,
        prefix_keys,
        prefix_values,
        kv_weight,
        prefix_states,
        norm_gain,
        segment_ids,
        segment_prompt,
        block_table,
    ):
        head_width = suffix_keys.shape[2]
        kv_local = head_width // HEAD_SIZE
        rows_local = prefix_keys.shape[1]
        pooled_rows = rows_local * n_smp * n_ten
        block_rows = rows_local * n_ten
        tok_count = queries.shape[1]
        group_size = queries.shape[2] // head_width
        visible = visible_keys(segment_ids[0], segment_prompt[0], block_table, pooled_rows)
        query_rows = queries[0].reshape(tok_count, kv_local, group_size, HEAD_SIZE)
        grad_rows = output_grad[0].reshape(tok_count, kv_local, group_size, HEAD_SIZE)
        own_keys = suffix_keys[0]
        own_values = suffix_values[0]
        pk = prefix_keys[0].reshape(rows_local, n_ten, kv_local, 1, HEAD_SIZE)
        pv = prefix_values[0].reshape(rows_local, n_ten, kv_local, 1, HEAD_SIZE)
        send = jnp.concatenate([pk, pv], axis=3).reshape(rows_local, n_ten, -1).transpose(1, 0, 2)
        got_all = lax.all_to_all(send, "tensor", 0, 0, tiled=True)
        got_all = got_all.reshape(block_rows, kv_local, 2 * HEAD_SIZE)

        query_pieces, suffix_key_pieces, suffix_value_pieces, reduced_pieces = [], [], [], []
        for head_index in range(kv_local):
            low_col = head_index * HEAD_SIZE
            got = got_all[:, head_index]
            if head_index % 2 == 0:
                spread = jnp.broadcast_to(got[None], (n_smp,) + got.shape)
                pool = lax.all_to_all(spread, "sample", 0, 0, tiled=True).reshape(pooled_rows, -1)
            else:
                pool = lax.all_gather(got, "sample", axis=0, tiled=True)
            key_rows = jnp.concatenate(
                [pool[:, :HEAD_SIZE], own_keys[:, low_col : low_col + HEAD_SIZE]], axis=0
            )
            value_rows = jnp.concatenate(
                [pool[:, HEAD_SIZE:], own_values[:, low_col : low_col + HEAD_SIZE]], axis=0
            )
            query_out, key_result, value_out = attend_group(
                query_rows[:, head_index], grad_rows[:, head_index], key_rows, value_rows, visible
            )
            query_pieces.append(query_out)
            suffix_key_pieces.append(key_result[pooled_rows:])
            suffix_value_pieces.append(value_out[pooled_rows:])
            pool_grad = jnp.concatenate(
                [key_result[:pooled_rows], value_out[:pooled_rows]], axis=1
            ).astype(jnp.bfloat16)
            pool_grad = pool_grad.reshape(n_smp, block_rows, 2 * HEAD_SIZE)
            parts = lax.all_to_all(pool_grad, "sample", 0, 0, tiled=False)
            reduced_pieces.append(jnp.sum(parts.astype(jnp.float32), axis=0))
        query_grad = jnp.stack(query_pieces, axis=1).reshape(tok_count, -1).astype(jnp.bfloat16)
        rollout_key_gradient = jnp.concatenate(suffix_key_pieces, axis=1).astype(jnp.bfloat16)
        suffix_value_grad = jnp.concatenate(suffix_value_pieces, axis=1).astype(jnp.bfloat16)

        reduced = jnp.concatenate(reduced_pieces, axis=1).astype(jnp.bfloat16)
        home_send = reduced.reshape(n_ten, rows_local, kv_local * 2 * HEAD_SIZE)
        home = lax.all_to_all(home_send, "tensor", 0, 0, tiled=True)
        home = home.reshape(n_ten, rows_local, kv_local, 2, HEAD_SIZE).transpose(3, 1, 0, 2, 4)
        home = home.reshape(2, rows_local, n_ten * kv_local * HEAD_SIZE).astype(jnp.float32)
        key_home = home[0]
        value_home = home[1]

        grad_cols = reduced.reshape(block_rows, kv_local, 2, HEAD_SIZE).transpose(0, 2, 1, 3)
        grad_cols = grad_cols.reshape(block_rows, 2, kv_local * HEAD_SIZE)
        group_term = lax.dot_general(
            grad_cols, kv_weight[0], (((1, 2), (1, 2)), ((), ())), preferred_element_type=jnp.float32
        ).astype(jnp.bfloat16)
        key_home, value_home, group_term = lax.optimization_barrier((key_home, value_home, group_term))
        width = group_term.shape[1]
        t_idx = lax.axis_index("tensor")
        core = t_idx % 2
        hi = t_idx // 2
        term4 = group_term.reshape(2, 2, rows_local, width)
        keep = lax.dynamic_index_in_dim(term4, core, 1, False)
        give = lax.dynamic_index_in_dim(term4, 1 - core, 1, False)
        core_pairs = [(i, i ^ 1) for i in range(n_ten)]
        chip_pairs = [(i, i ^ 2) for i in range(n_ten)]
        states_all = prefix_states[0]
        gain_wide = norm_gain[0].astype(jnp.float32)[None, :]
        sec = lax.axis_index("section")
        got1 = lax.ppermute(give, "tensor", core_pairs)
        partial = keep.astype(jnp.float32) + got1.astype(jnp.float32)
        mine_all = lax.dynamic_index_in_dim(partial, hi, 0, False)
        other_all = lax.dynamic_index_in_dim(partial, 1 - hi, 0, False).astype(jnp.bfloat16)
        n_chunks = 4
        step = rows_local // n_chunks
        outs = []
        previous = None
        for c in range(n_chunks):
            rows = slice(c * step, (c + 1) * step)
            other = other_all[rows]
            if previous is not None:
                other, previous = lax.optimization_barrier((other, previous))
            got2 = lax.ppermute(other, "tensor", chip_pairs)
            normed_grad = mine_all[rows] + got2.astype(jnp.float32)

            states = states_all[rows].astype(jnp.float32)
            inv_rms = lax.rsqrt(jnp.mean(states * states, axis=1, keepdims=True) + EPSILON)
            gained = gain_wide * normed_grad
            layer_term = inv_rms * gained - states * inv_rms**3 * jnp.mean(
                states * gained, axis=1, keepdims=True
            )
            term_low = layer_term.astype(jnp.bfloat16)
            previous = term_low
            if n_sec == 4:
                down = lax.ppermute(term_low, "section", [(3, 2), (2, 1)])
                wrap = lax.ppermute(term_low, "section", [(3, 0)])
                carry = (
                    jnp.where(sec == 1, layer_term, 0.0)
                    + down.astype(jnp.float32)
                    + wrap.astype(jnp.float32)
                )
                last = lax.ppermute(carry.astype(jnp.bfloat16), "section", [(1, 0), (0, 1)])
                outs.append(
                    layer_term
                    + down.astype(jnp.float32)
                    + wrap.astype(jnp.float32)
                    + last.astype(jnp.float32)
                )
            else:
                terms = lax.all_gather(term_low, "section")
                above = jnp.arange(n_sec) > sec
                outs.append(
                    layer_term
                    + jnp.sum(jnp.where(above[:, None, None], terms.astype(jnp.float32), 0.0), axis=0)
                )
        prefix_state_gradient = jnp.concatenate(outs, axis=0)
        return (
            query_grad[None],
            rollout_key_gradient[None],
            suffix_value_grad[None],
            key_home[None],
            value_home[None],
            prefix_state_gradient[None],
        )

    return on_device


def solution(mesh):
    placed = (
        P("section", "sample", "tensor"),
        P("section", "sample", "tensor"),
        P("section", "sample", "tensor"),
        P("section", "sample", "tensor"),
        P("section", ("sample", "tensor"), None),
        P("section", ("sample", "tensor"), None),
        P("section", None, None, "tensor"),
        P("section", ("sample", "tensor"), None),
        P("section", None),
        P("sample", None),
        P("sample", None),
        P(),
    )
    body = make_body(mesh.shape["section"], mesh.shape["sample"], mesh.shape["tensor"])
    return jax.shard_map(
        body,
        mesh=mesh,
        in_specs=placed,
        out_specs=(
            P("section", "sample", "tensor"),
            P("section", "sample", "tensor"),
            P("section", "sample", "tensor"),
            P("section", ("sample", "tensor"), None),
            P("section", ("sample", "tensor"), None),
            P("section", ("sample", "tensor"), None),
        ),
        check_vma=False,
    )
```

```python
import jax
import jax.numpy as jnp
from jax import lax
from jax.sharding import PartitionSpec as P

HEAD_SIZE = 128
PAGE = 128


MASKED_SCORE = -1e30
EPSILON = 1e-05


def visible_keys(seg_row, prompt_row, table, pooled_rows):
    tok_count = seg_row.shape[0]
    seg_hot = seg_row[:, None] == jnp.arange(prompt_row.shape[0], dtype=jnp.int32)[None, :]
    prompt_tok = jnp.sum(jnp.where(seg_hot, prompt_row[None, :], 0), axis=1)
    page_ids = jnp.arange(pooled_rows // PAGE, dtype=jnp.int32)
    member = jnp.any(table[:, :, None] == page_ids[None, None, :], axis=1)
    prompt_hot = prompt_tok[:, None] == jnp.arange(table.shape[0], dtype=jnp.int32)[None, :]
    member_tok = jnp.any(prompt_hot[:, :, None] & member[None, :, :], axis=1)
    prefix_seen = jnp.repeat(member_tok, PAGE, axis=1)
    position = jnp.arange(tok_count, dtype=jnp.int32)
    suffix_seen = (seg_row[:, None] == seg_row[None, :]) & (position[None, :] <= position[:, None])
    return jnp.concatenate([prefix_seen, suffix_seen], axis=1)


def attend_group(query_grp, grad_grp, key_rows, value_rows, visible):
    inv_root = query_grp.shape[-1] ** (-0.5)
    scores = (
        jnp.einsum("rgd,kd->rgk", query_grp, key_rows, preferred_element_type=jnp.float32)
        * inv_root
    )
    scores = jnp.where(visible[:, None, :], scores, MASKED_SCORE)
    row_max = jnp.max(scores, axis=2, keepdims=True)
    exponent = jnp.exp(scores - row_max)
    softmax_w = exponent / jnp.sum(exponent, axis=2, keepdims=True)
    weights_low = softmax_w.astype(jnp.bfloat16)
    attended = jnp.einsum(
        "rgk,kd->rgd", weights_low, value_rows, preferred_element_type=jnp.float32
    )
    delta_row = jnp.sum(grad_grp.astype(jnp.float32) * attended, axis=2, keepdims=True)
    weight_grad = jnp.einsum(
        "rgd,kd->rgk", grad_grp, value_rows, preferred_element_type=jnp.float32
    )
    score_grad = (softmax_w * (weight_grad - delta_row)).astype(jnp.bfloat16)
    query_out = (
        jnp.einsum("rgk,kd->rgd", score_grad, key_rows, preferred_element_type=jnp.float32)
        * inv_root
    )
    key_result = (
        jnp.einsum("rgk,rgd->kd", score_grad, query_grp, preferred_element_type=jnp.float32)
        * inv_root
    )
    value_out = jnp.einsum("rgk,rgd->kd", weights_low, grad_grp, preferred_element_type=jnp.float32)
    return (query_out, key_result, value_out)


def make_body(n_sec, n_smp, n_ten):
    def on_device(
        queries,
        suffix_keys,
        suffix_values,
        output_grad,
        prefix_keys,
        prefix_values,
        kv_weight,
        prefix_states,
        norm_gain,
        segment_ids,
        segment_prompt,
        block_table,
    ):
        head_width = suffix_keys.shape[2]
        kv_local = head_width // HEAD_SIZE
        rows_local = prefix_keys.shape[1]
        pooled_rows = rows_local * n_smp * n_ten
        block_rows = rows_local * n_ten
        tok_count = queries.shape[1]
        group_size = queries.shape[2] // head_width
        visible = visible_keys(segment_ids[0], segment_prompt[0], block_table, pooled_rows)
        query_rows = queries[0].reshape(tok_count, kv_local, group_size, HEAD_SIZE)
        grad_rows = output_grad[0].reshape(tok_count, kv_local, group_size, HEAD_SIZE)
        own_keys = suffix_keys[0]
        own_values = suffix_values[0]
        pk = prefix_keys[0].reshape(rows_local, n_ten, kv_local, 1, HEAD_SIZE)
        pv = prefix_values[0].reshape(rows_local, n_ten, kv_local, 1, HEAD_SIZE)
        send = jnp.concatenate([pk, pv], axis=3).reshape(rows_local, n_ten, -1).transpose(1, 0, 2)
        got_all = lax.all_to_all(send, "tensor", 0, 0, tiled=True)
        got_all = got_all.reshape(block_rows, kv_local, 2 * HEAD_SIZE)

        query_pieces, suffix_key_pieces, suffix_value_pieces, reduced_pieces = [], [], [], []
        for head_index in range(kv_local):
            low_col = head_index * HEAD_SIZE
            got = got_all[:, head_index]
            if head_index % 2 == 0:
                spread = jnp.broadcast_to(got[None], (n_smp,) + got.shape)
                pool = lax.all_to_all(spread, "sample", 0, 0, tiled=True).reshape(pooled_rows, -1)
            else:
                pool = lax.all_gather(got, "sample", axis=0, tiled=True)
            key_rows = jnp.concatenate(
                [pool[:, :HEAD_SIZE], own_keys[:, low_col : low_col + HEAD_SIZE]], axis=0
            )
            value_rows = jnp.concatenate(
                [pool[:, HEAD_SIZE:], own_values[:, low_col : low_col + HEAD_SIZE]], axis=0
            )
            query_out, key_result, value_out = attend_group(
                query_rows[:, head_index], grad_rows[:, head_index], key_rows, value_rows, visible
            )
            query_pieces.append(query_out)
            suffix_key_pieces.append(key_result[pooled_rows:])
            suffix_value_pieces.append(value_out[pooled_rows:])
            pool_grad = jnp.concatenate(
                [key_result[:pooled_rows], value_out[:pooled_rows]], axis=1
            ).astype(jnp.bfloat16)
            pool_grad = pool_grad.reshape(n_smp, block_rows, 2 * HEAD_SIZE)
            parts = lax.all_to_all(pool_grad, "sample", 0, 0, tiled=False)
            reduced_pieces.append(jnp.sum(parts.astype(jnp.float32), axis=0))
        query_grad = jnp.stack(query_pieces, axis=1).reshape(tok_count, -1).astype(jnp.bfloat16)
        rollout_key_gradient = jnp.concatenate(suffix_key_pieces, axis=1).astype(jnp.bfloat16)
        suffix_value_grad = jnp.concatenate(suffix_value_pieces, axis=1).astype(jnp.bfloat16)

        reduced = jnp.concatenate(reduced_pieces, axis=1).astype(jnp.bfloat16)
        home_send = reduced.reshape(n_ten, rows_local, kv_local * 2 * HEAD_SIZE)
        home = lax.all_to_all(home_send, "tensor", 0, 0, tiled=True)
        home = home.reshape(n_ten, rows_local, kv_local, 2, HEAD_SIZE).transpose(3, 1, 0, 2, 4)
        home = home.reshape(2, rows_local, n_ten * kv_local * HEAD_SIZE).astype(jnp.float32)
        key_home = home[0]
        value_home = home[1]

        grad_cols = reduced.reshape(block_rows, kv_local, 2, HEAD_SIZE).transpose(0, 2, 1, 3)
        grad_cols = grad_cols.reshape(n_ten, rows_local, 2, kv_local * HEAD_SIZE)
        weight_local = kv_weight[0]
        width = weight_local.shape[0]
        t_idx = lax.axis_index("tensor")
        core = t_idx % 2
        hi = t_idx // 2
        core_pairs = [(i, i ^ 1) for i in range(n_ten)]
        chip_pairs = [(i, i ^ 2) for i in range(n_ten)]
        states_all = prefix_states[0]
        gain_wide = norm_gain[0].astype(jnp.float32)[None, :]
        sec = lax.axis_index("section")
        n_chunks = 4
        step = rows_local // n_chunks
        outs = []
        previous = None
        for c in range(n_chunks):
            rows = slice(c * step, (c + 1) * step)
            grad_rows_c = grad_cols[:, rows]
            if c > 0:
                grad_rows_c, sent = lax.optimization_barrier((grad_rows_c, sent))
            group_term = lax.dot_general(
                grad_rows_c, weight_local, (((2, 3), (1, 2)), ((), ())),
                preferred_element_type=jnp.float32,
            ).astype(jnp.bfloat16)
            if c == 0:
                key_home, value_home, group_term = lax.optimization_barrier(
                    (key_home, value_home, group_term)
                )
            term4 = group_term.reshape(2, 2, step, width)
            keep = lax.dynamic_index_in_dim(term4, core, 1, False)
            give = lax.dynamic_index_in_dim(term4, 1 - core, 1, False)
            got1 = lax.ppermute(give, "tensor", core_pairs)
            partial = keep.astype(jnp.float32) + got1.astype(jnp.float32)
            mine = lax.dynamic_index_in_dim(partial, hi, 0, False)
            other = lax.dynamic_index_in_dim(partial, 1 - hi, 0, False).astype(jnp.bfloat16)
            if previous is not None:
                other, previous = lax.optimization_barrier((other, previous))
            sent = other
            got2 = lax.ppermute(other, "tensor", chip_pairs)
            normed_grad = mine + got2.astype(jnp.float32)

            states = states_all[rows].astype(jnp.float32)
            inv_rms = lax.rsqrt(jnp.mean(states * states, axis=1, keepdims=True) + EPSILON)
            gained = gain_wide * normed_grad
            layer_term = inv_rms * gained - states * inv_rms**3 * jnp.mean(
                states * gained, axis=1, keepdims=True
            )
            term_low = layer_term.astype(jnp.bfloat16)
            previous = term_low
            if n_sec == 4:
                down = lax.ppermute(term_low, "section", [(3, 2), (2, 1)])
                wrap = lax.ppermute(term_low, "section", [(3, 0)])
                carry = (
                    jnp.where(sec == 1, layer_term, 0.0)
                    + down.astype(jnp.float32)
                    + wrap.astype(jnp.float32)
                )
                last = lax.ppermute(carry.astype(jnp.bfloat16), "section", [(1, 0), (0, 1)])
                outs.append(
                    layer_term
                    + down.astype(jnp.float32)
                    + wrap.astype(jnp.float32)
                    + last.astype(jnp.float32)
                )
            else:
                terms = lax.all_gather(term_low, "section")
                above = jnp.arange(n_sec) > sec
                outs.append(
                    layer_term
                    + jnp.sum(jnp.where(above[:, None, None], terms.astype(jnp.float32), 0.0), axis=0)
                )
        prefix_state_gradient = jnp.concatenate(outs, axis=0)
        return (
            query_grad[None],
            rollout_key_gradient[None],
            suffix_value_grad[None],
            key_home[None],
            value_home[None],
            prefix_state_gradient[None],
        )

    return on_device


def solution(mesh):
    placed = (
        P("section", "sample", "tensor"),
        P("section", "sample", "tensor"),
        P("section", "sample", "tensor"),
        P("section", "sample", "tensor"),
        P("section", ("sample", "tensor"), None),
        P("section", ("sample", "tensor"), None),
        P("section", None, None, "tensor"),
        P("section", ("sample", "tensor"), None),
        P("section", None),
        P("sample", None),
        P("sample", None),
        P(),
    )
    body = make_body(mesh.shape["section"], mesh.shape["sample"], mesh.shape["tensor"])
    return jax.shard_map(
        body,
        mesh=mesh,
        in_specs=placed,
        out_specs=(
            P("section", "sample", "tensor"),
            P("section", "sample", "tensor"),
            P("section", "sample", "tensor"),
            P("section", ("sample", "tensor"), None),
            P("section", ("sample", "tensor"), None),
            P("section", ("sample", "tensor"), None),
        ),
        check_vma=False,
    )
```

```python
import jax
import jax.numpy as jnp
from jax import lax
from jax.sharding import PartitionSpec as P

HEAD_SIZE = 128
PAGE = 128


MASKED_SCORE = -1e30
EPSILON = 1e-05


def visible_keys(seg_row, prompt_row, table, pooled_rows):
    tok_count = seg_row.shape[0]
    seg_hot = seg_row[:, None] == jnp.arange(prompt_row.shape[0], dtype=jnp.int32)[None, :]
    prompt_tok = jnp.sum(jnp.where(seg_hot, prompt_row[None, :], 0), axis=1)
    page_ids = jnp.arange(pooled_rows // PAGE, dtype=jnp.int32)
    member = jnp.any(table[:, :, None] == page_ids[None, None, :], axis=1)
    prompt_hot = prompt_tok[:, None] == jnp.arange(table.shape[0], dtype=jnp.int32)[None, :]
    member_tok = jnp.any(prompt_hot[:, :, None] & member[None, :, :], axis=1)
    prefix_seen = jnp.repeat(member_tok, PAGE, axis=1)
    position = jnp.arange(tok_count, dtype=jnp.int32)
    suffix_seen = (seg_row[:, None] == seg_row[None, :]) & (position[None, :] <= position[:, None])
    return jnp.concatenate([prefix_seen, suffix_seen], axis=1)


def attend_group(query_grp, grad_grp, key_rows, value_rows, visible):
    inv_root = query_grp.shape[-1] ** (-0.5)
    scores = (
        jnp.einsum("rgd,kd->rgk", query_grp, key_rows, preferred_element_type=jnp.float32)
        * inv_root
    )
    scores = jnp.where(visible[:, None, :], scores, MASKED_SCORE)
    row_max = jnp.max(scores, axis=2, keepdims=True)
    exponent = jnp.exp(scores - row_max)
    softmax_w = exponent / jnp.sum(exponent, axis=2, keepdims=True)
    weights_low = softmax_w.astype(jnp.bfloat16)
    attended = jnp.einsum(
        "rgk,kd->rgd", weights_low, value_rows, preferred_element_type=jnp.float32
    )
    delta_row = jnp.sum(grad_grp.astype(jnp.float32) * attended, axis=2, keepdims=True)
    weight_grad = jnp.einsum(
        "rgd,kd->rgk", grad_grp, value_rows, preferred_element_type=jnp.float32
    )
    score_grad = (softmax_w * (weight_grad - delta_row)).astype(jnp.bfloat16)
    key_result = (
        jnp.einsum("rgk,rgd->kd", score_grad, query_grp, preferred_element_type=jnp.float32)
        * inv_root
    )
    value_out = jnp.einsum("rgk,rgd->kd", weights_low, grad_grp, preferred_element_type=jnp.float32)
    return (score_grad, key_result, value_out)


def make_body(n_sec, n_smp, n_ten):
    def on_device(
        queries,
        suffix_keys,
        suffix_values,
        output_grad,
        prefix_keys,
        prefix_values,
        kv_weight,
        prefix_states,
        norm_gain,
        segment_ids,
        segment_prompt,
        block_table,
    ):
        head_width = suffix_keys.shape[2]
        kv_local = head_width // HEAD_SIZE
        rows_local = prefix_keys.shape[1]
        pooled_rows = rows_local * n_smp * n_ten
        block_rows = rows_local * n_ten
        tok_count = queries.shape[1]
        group_size = queries.shape[2] // head_width
        visible = visible_keys(segment_ids[0], segment_prompt[0], block_table, pooled_rows)
        query_rows = queries[0].reshape(tok_count, kv_local, group_size, HEAD_SIZE)
        grad_rows = output_grad[0].reshape(tok_count, kv_local, group_size, HEAD_SIZE)
        own_keys = suffix_keys[0]
        own_values = suffix_values[0]
        pk = prefix_keys[0].reshape(rows_local, n_ten, kv_local, 1, HEAD_SIZE)
        pv = prefix_values[0].reshape(rows_local, n_ten, kv_local, 1, HEAD_SIZE)
        send = jnp.concatenate([pk, pv], axis=3).reshape(rows_local, n_ten, -1).transpose(1, 0, 2)
        got_all = lax.all_to_all(send, "tensor", 0, 0, tiled=True)
        got_all = got_all.reshape(block_rows, kv_local, 2 * HEAD_SIZE)

        query_pieces, suffix_key_pieces, suffix_value_pieces, reduced_pieces = [], [], [], []
        for head_index in range(kv_local):
            low_col = head_index * HEAD_SIZE
            got = got_all[:, head_index]
            if head_index % 2 == 0:
                spread = jnp.broadcast_to(got[None], (n_smp,) + got.shape)
                pool = lax.all_to_all(spread, "sample", 0, 0, tiled=True).reshape(pooled_rows, -1)
            else:
                got, _ = lax.optimization_barrier((got, pool))
                pool = lax.all_gather(got, "sample", axis=0, tiled=True)
            key_rows = jnp.concatenate(
                [pool[:, :HEAD_SIZE], own_keys[:, low_col : low_col + HEAD_SIZE]], axis=0
            )
            value_rows = jnp.concatenate(
                [pool[:, HEAD_SIZE:], own_values[:, low_col : low_col + HEAD_SIZE]], axis=0
            )
            score_grad, key_result, value_out = attend_group(
                query_rows[:, head_index], grad_rows[:, head_index], key_rows, value_rows, visible
            )
            suffix_key_pieces.append(key_result[pooled_rows:])
            suffix_value_pieces.append(value_out[pooled_rows:])
            pool_grad = jnp.concatenate(
                [key_result[:pooled_rows], value_out[:pooled_rows]], axis=1
            ).astype(jnp.bfloat16)
            pool_grad = pool_grad.reshape(n_smp, block_rows, 2 * HEAD_SIZE)
            score_grad, pool_grad = lax.optimization_barrier((score_grad, pool_grad))
            query_pieces.append(
                jnp.einsum("rgk,kd->rgd", score_grad, key_rows, preferred_element_type=jnp.float32)
                * HEAD_SIZE ** (-0.5)
            )
            parts = lax.all_to_all(pool_grad, "sample", 0, 0, tiled=False)
            reduced_pieces.append(jnp.sum(parts.astype(jnp.float32), axis=0))
        query_grad = jnp.stack(query_pieces, axis=1).reshape(tok_count, -1).astype(jnp.bfloat16)
        rollout_key_gradient = jnp.concatenate(suffix_key_pieces, axis=1).astype(jnp.bfloat16)
        suffix_value_grad = jnp.concatenate(suffix_value_pieces, axis=1).astype(jnp.bfloat16)

        reduced = jnp.concatenate(reduced_pieces, axis=1).astype(jnp.bfloat16)
        home_send = reduced.reshape(n_ten, rows_local, kv_local * 2 * HEAD_SIZE)
        home = lax.all_to_all(home_send, "tensor", 0, 0, tiled=True)
        home = home.reshape(n_ten, rows_local, kv_local, 2, HEAD_SIZE).transpose(3, 1, 0, 2, 4)
        home = home.reshape(2, rows_local, n_ten * kv_local * HEAD_SIZE).astype(jnp.float32)
        key_home = home[0]
        value_home = home[1]

        grad_cols = reduced.reshape(block_rows, kv_local, 2, HEAD_SIZE).transpose(0, 2, 1, 3)
        grad_cols = grad_cols.reshape(n_ten, rows_local, 2, kv_local * HEAD_SIZE)
        weight_local = kv_weight[0]
        width = weight_local.shape[0]
        t_idx = lax.axis_index("tensor")
        core = t_idx % 2
        hi = t_idx // 2
        core_pairs = [(i, i ^ 1) for i in range(n_ten)]
        chip_pairs = [(i, i ^ 2) for i in range(n_ten)]
        states_all = prefix_states[0]
        gain_wide = norm_gain[0].astype(jnp.float32)[None, :]
        sec = lax.axis_index("section")
        n_chunks = 4
        step = rows_local // n_chunks
        outs = []
        previous = None
        for c in range(n_chunks):
            rows = slice(c * step, (c + 1) * step)
            grad_rows_c = grad_cols[:, rows]
            if c > 0:
                grad_rows_c, sent = lax.optimization_barrier((grad_rows_c, sent))
            group_term = lax.dot_general(
                grad_rows_c, weight_local, (((2, 3), (1, 2)), ((), ())),
                preferred_element_type=jnp.float32,
            ).astype(jnp.bfloat16)
            if c == 0:
                key_home, value_home, group_term = lax.optimization_barrier(
                    (key_home, value_home, group_term)
                )
            term4 = group_term.reshape(2, 2, step, width)
            keep = lax.dynamic_index_in_dim(term4, core, 1, False)
            give = lax.dynamic_index_in_dim(term4, 1 - core, 1, False)
            got1 = lax.ppermute(give, "tensor", core_pairs)
            partial = keep.astype(jnp.float32) + got1.astype(jnp.float32)
            mine = lax.dynamic_index_in_dim(partial, hi, 0, False)
            other = lax.dynamic_index_in_dim(partial, 1 - hi, 0, False).astype(jnp.bfloat16)
            if previous is not None:
                other, previous = lax.optimization_barrier((other, previous))
            sent = other
            got2 = lax.ppermute(other, "tensor", chip_pairs)
            normed_grad = mine + got2.astype(jnp.float32)

            states = states_all[rows].astype(jnp.float32)
            inv_rms = lax.rsqrt(jnp.mean(states * states, axis=1, keepdims=True) + EPSILON)
            gained = gain_wide * normed_grad
            layer_term = inv_rms * gained - states * inv_rms**3 * jnp.mean(
                states * gained, axis=1, keepdims=True
            )
            term_low = layer_term.astype(jnp.bfloat16)
            previous = term_low
            if n_sec == 4:
                down = lax.ppermute(term_low, "section", [(3, 2), (2, 1)])
                wrap = lax.ppermute(term_low, "section", [(3, 0)])
                carry = (
                    jnp.where(sec == 1, layer_term, 0.0)
                    + down.astype(jnp.float32)
                    + wrap.astype(jnp.float32)
                )
                last = lax.ppermute(carry.astype(jnp.bfloat16), "section", [(1, 0), (0, 1)])
                outs.append(
                    layer_term
                    + down.astype(jnp.float32)
                    + wrap.astype(jnp.float32)
                    + last.astype(jnp.float32)
                )
            else:
                terms = lax.all_gather(term_low, "section")
                above = jnp.arange(n_sec) > sec
                outs.append(
                    layer_term
                    + jnp.sum(jnp.where(above[:, None, None], terms.astype(jnp.float32), 0.0), axis=0)
                )
        prefix_state_gradient = jnp.concatenate(outs, axis=0)
        return (
            query_grad[None],
            rollout_key_gradient[None],
            suffix_value_grad[None],
            key_home[None],
            value_home[None],
            prefix_state_gradient[None],
        )

    return on_device


def solution(mesh):
    placed = (
        P("section", "sample", "tensor"),
        P("section", "sample", "tensor"),
        P("section", "sample", "tensor"),
        P("section", "sample", "tensor"),
        P("section", ("sample", "tensor"), None),
        P("section", ("sample", "tensor"), None),
        P("section", None, None, "tensor"),
        P("section", ("sample", "tensor"), None),
        P("section", None),
        P("sample", None),
        P("sample", None),
        P(),
    )
    body = make_body(mesh.shape["section"], mesh.shape["sample"], mesh.shape["tensor"])
    return jax.shard_map(
        body,
        mesh=mesh,
        in_specs=placed,
        out_specs=(
            P("section", "sample", "tensor"),
            P("section", "sample", "tensor"),
            P("section", "sample", "tensor"),
            P("section", ("sample", "tensor"), None),
            P("section", ("sample", "tensor"), None),
            P("section", ("sample", "tensor"), None),
        ),
        check_vma=False,
    )
```

```python
import jax
import jax.numpy as jnp
from jax import lax
from jax.sharding import PartitionSpec as P

HEAD_SIZE = 128
PAGE = 128


MASKED_SCORE = -1e30
EPSILON = 1e-05


def visible_keys(seg_row, prompt_row, table, pooled_rows):
    tok_count = seg_row.shape[0]
    seg_hot = seg_row[:, None] == jnp.arange(prompt_row.shape[0], dtype=jnp.int32)[None, :]
    prompt_tok = jnp.sum(jnp.where(seg_hot, prompt_row[None, :], 0), axis=1)
    page_ids = jnp.arange(pooled_rows // PAGE, dtype=jnp.int32)
    member = jnp.any(table[:, :, None] == page_ids[None, None, :], axis=1)
    prompt_hot = prompt_tok[:, None] == jnp.arange(table.shape[0], dtype=jnp.int32)[None, :]
    member_tok = jnp.any(prompt_hot[:, :, None] & member[None, :, :], axis=1)
    prefix_seen = jnp.repeat(member_tok, PAGE, axis=1)
    position = jnp.arange(tok_count, dtype=jnp.int32)
    suffix_seen = (seg_row[:, None] == seg_row[None, :]) & (position[None, :] <= position[:, None])
    return jnp.concatenate([prefix_seen, suffix_seen], axis=1)


def attend_group(query_grp, grad_grp, key_rows, value_rows, visible):
    inv_root = query_grp.shape[-1] ** (-0.5)
    scores = (
        jnp.einsum("rgd,kd->rgk", query_grp, key_rows, preferred_element_type=jnp.float32)
        * inv_root
    )
    scores = jnp.where(visible[:, None, :], scores, MASKED_SCORE)
    row_max = jnp.max(scores, axis=2, keepdims=True)
    exponent = jnp.exp(scores - row_max)
    softmax_w = exponent / jnp.sum(exponent, axis=2, keepdims=True)
    weights_low = softmax_w.astype(jnp.bfloat16)
    attended = jnp.einsum(
        "rgk,kd->rgd", weights_low, value_rows, preferred_element_type=jnp.float32
    )
    delta_row = jnp.sum(grad_grp.astype(jnp.float32) * attended, axis=2, keepdims=True)
    weight_grad = jnp.einsum(
        "rgd,kd->rgk", grad_grp, value_rows, preferred_element_type=jnp.float32
    )
    score_grad = (softmax_w * (weight_grad - delta_row)).astype(jnp.bfloat16)
    key_result = (
        jnp.einsum("rgk,rgd->kd", score_grad, query_grp, preferred_element_type=jnp.float32)
        * inv_root
    )
    value_out = jnp.einsum("rgk,rgd->kd", weights_low, grad_grp, preferred_element_type=jnp.float32)
    return (score_grad, key_result, value_out)


def make_body(n_sec, n_smp, n_ten):
    def on_device(
        queries,
        suffix_keys,
        suffix_values,
        output_grad,
        prefix_keys,
        prefix_values,
        kv_weight,
        prefix_states,
        norm_gain,
        segment_ids,
        segment_prompt,
        block_table,
    ):
        head_width = suffix_keys.shape[2]
        kv_local = head_width // HEAD_SIZE
        rows_local = prefix_keys.shape[1]
        pooled_rows = rows_local * n_smp * n_ten
        block_rows = rows_local * n_ten
        tok_count = queries.shape[1]
        group_size = queries.shape[2] // head_width
        visible = visible_keys(segment_ids[0], segment_prompt[0], block_table, pooled_rows)
        query_rows = queries[0].reshape(tok_count, kv_local, group_size, HEAD_SIZE)
        grad_rows = output_grad[0].reshape(tok_count, kv_local, group_size, HEAD_SIZE)
        own_keys = suffix_keys[0]
        own_values = suffix_values[0]
        pk = prefix_keys[0].reshape(rows_local, n_ten, kv_local, 1, HEAD_SIZE)
        pv = prefix_values[0].reshape(rows_local, n_ten, kv_local, 1, HEAD_SIZE)
        send = jnp.concatenate([pk, pv], axis=3).reshape(rows_local, n_ten, -1).transpose(1, 0, 2)
        got_all = lax.all_to_all(send, "tensor", 0, 0, tiled=True)
        got_all = got_all.reshape(block_rows, kv_local, 2 * HEAD_SIZE)

        query_pieces, suffix_key_pieces, suffix_value_pieces, reduced_pieces = [], [], [], []
        for head_index in range(kv_local):
            low_col = head_index * HEAD_SIZE
            got = got_all[:, head_index]
            if head_index % 2 == 0:
                spread = jnp.broadcast_to(got[None], (n_smp,) + got.shape)
                pool = lax.all_to_all(spread, "sample", 0, 0, tiled=True).reshape(pooled_rows, -1)
            else:
                got, _ = lax.optimization_barrier((got, pool))
                pool = lax.all_gather(got, "sample", axis=0, tiled=True)
            key_rows = jnp.concatenate(
                [pool[:, :HEAD_SIZE], own_keys[:, low_col : low_col + HEAD_SIZE]], axis=0
            )
            value_rows = jnp.concatenate(
                [pool[:, HEAD_SIZE:], own_values[:, low_col : low_col + HEAD_SIZE]], axis=0
            )
            score_grad, key_result, value_out = attend_group(
                query_rows[:, head_index], grad_rows[:, head_index], key_rows, value_rows, visible
            )
            suffix_key_pieces.append(key_result[pooled_rows:])
            suffix_value_pieces.append(value_out[pooled_rows:])
            pool_grad = jnp.concatenate(
                [key_result[:pooled_rows], value_out[:pooled_rows]], axis=1
            ).astype(jnp.bfloat16)
            pool_grad = pool_grad.reshape(n_smp, block_rows, 2 * HEAD_SIZE)
            score_grad, pool_grad = lax.optimization_barrier((score_grad, pool_grad))
            query_pieces.append(
                jnp.einsum("rgk,kd->rgd", score_grad, key_rows, preferred_element_type=jnp.float32)
                * HEAD_SIZE ** (-0.5)
            )
            parts = lax.all_to_all(pool_grad, "sample", 0, 0, tiled=False)
            reduced_pieces.append(jnp.sum(parts.astype(jnp.float32), axis=0))
        query_grad = jnp.stack(query_pieces, axis=1).reshape(tok_count, -1).astype(jnp.bfloat16)
        rollout_key_gradient = jnp.concatenate(suffix_key_pieces, axis=1).astype(jnp.bfloat16)
        suffix_value_grad = jnp.concatenate(suffix_value_pieces, axis=1).astype(jnp.bfloat16)

        reduced = jnp.concatenate(reduced_pieces, axis=1).astype(jnp.bfloat16)
        home_send = reduced.reshape(n_ten, rows_local, kv_local * 2 * HEAD_SIZE)
        home = lax.all_to_all(home_send, "tensor", 0, 0, tiled=True)
        home = home.reshape(n_ten, rows_local, kv_local, 2, HEAD_SIZE).transpose(3, 1, 0, 2, 4)
        home = home.reshape(2, rows_local, n_ten * kv_local * HEAD_SIZE).astype(jnp.float32)
        key_home = home[0]
        value_home = home[1]

        grad_cols = reduced.reshape(block_rows, kv_local, 2, HEAD_SIZE).transpose(0, 2, 1, 3)
        grad_cols = grad_cols.reshape(n_ten, rows_local, 2, kv_local * HEAD_SIZE)
        weight_local = kv_weight[0]
        width = weight_local.shape[0]
        t_idx = lax.axis_index("tensor")
        core = t_idx % 2
        hi = t_idx // 2
        core_pairs = [(i, i ^ 1) for i in range(n_ten)]
        chip_pairs = [(i, i ^ 2) for i in range(n_ten)]
        states_all = prefix_states[0]
        gain_wide = norm_gain[0].astype(jnp.float32)[None, :]
        sec = lax.axis_index("section")
        unit = rows_local // 8
        sizes = [3 * unit, 2 * unit, 2 * unit, unit]
        starts = [sum(sizes[:i]) for i in range(len(sizes))]
        outs = []
        previous = None
        for c in range(len(sizes)):
            step = sizes[c]
            rows = slice(starts[c], starts[c] + step)
            grad_rows_c = grad_cols[:, rows]
            if c > 0:
                grad_rows_c, sent = lax.optimization_barrier((grad_rows_c, sent))
            group_term = lax.dot_general(
                grad_rows_c, weight_local, (((2, 3), (1, 2)), ((), ())),
                preferred_element_type=jnp.float32,
            ).astype(jnp.bfloat16)
            if c == 0:
                key_home, value_home, group_term = lax.optimization_barrier(
                    (key_home, value_home, group_term)
                )
            term4 = group_term.reshape(2, 2, step, width)
            keep = lax.dynamic_index_in_dim(term4, core, 1, False)
            give = lax.dynamic_index_in_dim(term4, 1 - core, 1, False)
            got1 = lax.ppermute(give, "tensor", core_pairs)
            partial = keep.astype(jnp.float32) + got1.astype(jnp.float32)
            mine = lax.dynamic_index_in_dim(partial, hi, 0, False)
            other = lax.dynamic_index_in_dim(partial, 1 - hi, 0, False).astype(jnp.bfloat16)
            if previous is not None:
                other, previous = lax.optimization_barrier((other, previous))
            sent = other
            got2 = lax.ppermute(other, "tensor", chip_pairs)
            normed_grad = mine + got2.astype(jnp.float32)

            states = states_all[rows].astype(jnp.float32)
            inv_rms = lax.rsqrt(jnp.mean(states * states, axis=1, keepdims=True) + EPSILON)
            gained = gain_wide * normed_grad
            layer_term = inv_rms * gained - states * inv_rms**3 * jnp.mean(
                states * gained, axis=1, keepdims=True
            )
            term_low = layer_term.astype(jnp.bfloat16)
            previous = term_low
            if n_sec == 4:
                down = lax.ppermute(term_low, "section", [(3, 2), (2, 1)])
                wrap = lax.ppermute(term_low, "section", [(3, 0)])
                carry = (
                    jnp.where(sec == 1, layer_term, 0.0)
                    + down.astype(jnp.float32)
                    + wrap.astype(jnp.float32)
                )
                last = lax.ppermute(carry.astype(jnp.bfloat16), "section", [(1, 0), (0, 1)])
                outs.append(
                    layer_term
                    + down.astype(jnp.float32)
                    + wrap.astype(jnp.float32)
                    + last.astype(jnp.float32)
                )
            else:
                terms = lax.all_gather(term_low, "section")
                above = jnp.arange(n_sec) > sec
                outs.append(
                    layer_term
                    + jnp.sum(jnp.where(above[:, None, None], terms.astype(jnp.float32), 0.0), axis=0)
                )
        prefix_state_gradient = jnp.concatenate(outs, axis=0)
        return (
            query_grad[None],
            rollout_key_gradient[None],
            suffix_value_grad[None],
            key_home[None],
            value_home[None],
            prefix_state_gradient[None],
        )

    return on_device


def solution(mesh):
    placed = (
        P("section", "sample", "tensor"),
        P("section", "sample", "tensor"),
        P("section", "sample", "tensor"),
        P("section", "sample", "tensor"),
        P("section", ("sample", "tensor"), None),
        P("section", ("sample", "tensor"), None),
        P("section", None, None, "tensor"),
        P("section", ("sample", "tensor"), None),
        P("section", None),
        P("sample", None),
        P("sample", None),
        P(),
    )
    body = make_body(mesh.shape["section"], mesh.shape["sample"], mesh.shape["tensor"])
    return jax.shard_map(
        body,
        mesh=mesh,
        in_specs=placed,
        out_specs=(
            P("section", "sample", "tensor"),
            P("section", "sample", "tensor"),
            P("section", "sample", "tensor"),
            P("section", ("sample", "tensor"), None),
            P("section", ("sample", "tensor"), None),
            P("section", ("sample", "tensor"), None),
        ),
        check_vma=False,
    )
```

```python
import jax
import jax.numpy as jnp
from jax import lax
from jax.sharding import PartitionSpec as P

HEAD_SIZE = 128
PAGE = 128


MASKED_SCORE = -1e30
EPSILON = 1e-05


def visible_keys(seg_row, prompt_row, table, pooled_rows):
    tok_count = seg_row.shape[0]
    seg_hot = seg_row[:, None] == jnp.arange(prompt_row.shape[0], dtype=jnp.int32)[None, :]
    prompt_tok = jnp.sum(jnp.where(seg_hot, prompt_row[None, :], 0), axis=1)
    page_ids = jnp.arange(pooled_rows // PAGE, dtype=jnp.int32)
    member = jnp.any(table[:, :, None] == page_ids[None, None, :], axis=1)
    prompt_hot = prompt_tok[:, None] == jnp.arange(table.shape[0], dtype=jnp.int32)[None, :]
    member_tok = jnp.any(prompt_hot[:, :, None] & member[None, :, :], axis=1)
    prefix_seen = jnp.repeat(member_tok, PAGE, axis=1)
    position = jnp.arange(tok_count, dtype=jnp.int32)
    suffix_seen = (seg_row[:, None] == seg_row[None, :]) & (position[None, :] <= position[:, None])
    return jnp.concatenate([prefix_seen, suffix_seen], axis=1)


def attend_group(query_grp, grad_grp, key_rows, value_rows, visible):
    inv_root = query_grp.shape[-1] ** (-0.5)
    scores = (
        jnp.einsum("rgd,kd->rgk", query_grp, key_rows, preferred_element_type=jnp.float32)
        * inv_root
    )
    scores = jnp.where(visible[:, None, :], scores, MASKED_SCORE)
    row_max = jnp.max(scores, axis=2, keepdims=True)
    exponent = jnp.exp(scores - row_max)
    softmax_w = exponent / jnp.sum(exponent, axis=2, keepdims=True)
    weights_low = softmax_w.astype(jnp.bfloat16)
    attended = jnp.einsum(
        "rgk,kd->rgd", weights_low, value_rows, preferred_element_type=jnp.float32
    )
    delta_row = jnp.sum(grad_grp.astype(jnp.float32) * attended, axis=2, keepdims=True)
    weight_grad = jnp.einsum(
        "rgd,kd->rgk", grad_grp, value_rows, preferred_element_type=jnp.float32
    )
    score_grad = (softmax_w * (weight_grad - delta_row)).astype(jnp.bfloat16)
    key_result = (
        jnp.einsum("rgk,rgd->kd", score_grad, query_grp, preferred_element_type=jnp.float32)
        * inv_root
    )
    value_out = jnp.einsum("rgk,rgd->kd", weights_low, grad_grp, preferred_element_type=jnp.float32)
    return (score_grad, key_result, value_out)


def make_body(n_sec, n_smp, n_ten):
    def on_device(
        queries,
        suffix_keys,
        suffix_values,
        output_grad,
        prefix_keys,
        prefix_values,
        kv_weight,
        prefix_states,
        norm_gain,
        segment_ids,
        segment_prompt,
        block_table,
    ):
        head_width = suffix_keys.shape[2]
        kv_local = head_width // HEAD_SIZE
        rows_local = prefix_keys.shape[1]
        pooled_rows = rows_local * n_smp * n_ten
        block_rows = rows_local * n_ten
        tok_count = queries.shape[1]
        group_size = queries.shape[2] // head_width
        visible = visible_keys(segment_ids[0], segment_prompt[0], block_table, pooled_rows)
        query_rows = queries[0].reshape(tok_count, kv_local, group_size, HEAD_SIZE)
        grad_rows = output_grad[0].reshape(tok_count, kv_local, group_size, HEAD_SIZE)
        own_keys = suffix_keys[0]
        own_values = suffix_values[0]
        pk = prefix_keys[0].reshape(rows_local, n_ten, kv_local, 1, HEAD_SIZE)
        pv = prefix_values[0].reshape(rows_local, n_ten, kv_local, 1, HEAD_SIZE)
        send = jnp.concatenate([pk, pv], axis=3).reshape(rows_local, n_ten, kv_local, -1)
        send = send.transpose(2, 1, 0, 3)
        spread = jnp.broadcast_to(send[0][None], (n_smp,) + send[0].shape)
        spread = spread.reshape((n_smp * n_ten,) + send[0].shape[1:])
        first_pool = lax.all_to_all(spread, ("sample", "tensor"), 0, 0, tiled=True)
        first_pool = first_pool.reshape(pooled_rows, 2 * HEAD_SIZE)
        got_rest = lax.all_to_all(send[1:], "tensor", 1, 1, tiled=True)

        query_pieces, suffix_key_pieces, suffix_value_pieces, reduced_pieces = [], [], [], []
        for head_index in range(kv_local):
            low_col = head_index * HEAD_SIZE
            if head_index == 0:
                pool = first_pool
            else:
                got = got_rest[head_index - 1].reshape(block_rows, 2 * HEAD_SIZE)
                got, _ = lax.optimization_barrier((got, first_pool))
                pool = lax.all_gather(got, "sample", axis=0, tiled=True)
            key_rows = jnp.concatenate(
                [pool[:, :HEAD_SIZE], own_keys[:, low_col : low_col + HEAD_SIZE]], axis=0
            )
            value_rows = jnp.concatenate(
                [pool[:, HEAD_SIZE:], own_values[:, low_col : low_col + HEAD_SIZE]], axis=0
            )
            score_grad, key_result, value_out = attend_group(
                query_rows[:, head_index], grad_rows[:, head_index], key_rows, value_rows, visible
            )
            suffix_key_pieces.append(key_result[pooled_rows:])
            suffix_value_pieces.append(value_out[pooled_rows:])
            pool_grad = jnp.concatenate(
                [key_result[:pooled_rows], value_out[:pooled_rows]], axis=1
            ).astype(jnp.bfloat16)
            pool_grad = pool_grad.reshape(n_smp, block_rows, 2 * HEAD_SIZE)
            score_grad, pool_grad = lax.optimization_barrier((score_grad, pool_grad))
            query_pieces.append(
                jnp.einsum("rgk,kd->rgd", score_grad, key_rows, preferred_element_type=jnp.float32)
                * HEAD_SIZE ** (-0.5)
            )
            parts = lax.all_to_all(pool_grad, "sample", 0, 0, tiled=False)
            reduced_pieces.append(jnp.sum(parts.astype(jnp.float32), axis=0))
        query_grad = jnp.stack(query_pieces, axis=1).reshape(tok_count, -1).astype(jnp.bfloat16)
        rollout_key_gradient = jnp.concatenate(suffix_key_pieces, axis=1).astype(jnp.bfloat16)
        suffix_value_grad = jnp.concatenate(suffix_value_pieces, axis=1).astype(jnp.bfloat16)

        reduced = jnp.concatenate(reduced_pieces, axis=1).astype(jnp.bfloat16)
        home_send = reduced.reshape(n_ten, rows_local, kv_local * 2 * HEAD_SIZE)
        home = lax.all_to_all(home_send, "tensor", 0, 0, tiled=True)
        home = home.reshape(n_ten, rows_local, kv_local, 2, HEAD_SIZE).transpose(3, 1, 0, 2, 4)
        home = home.reshape(2, rows_local, n_ten * kv_local * HEAD_SIZE).astype(jnp.float32)
        key_home = home[0]
        value_home = home[1]

        grad_cols = reduced.reshape(block_rows, kv_local, 2, HEAD_SIZE).transpose(0, 2, 1, 3)
        grad_cols = grad_cols.reshape(n_ten, rows_local, 2, kv_local * HEAD_SIZE)
        weight_local = kv_weight[0]
        width = weight_local.shape[0]
        t_idx = lax.axis_index("tensor")
        core = t_idx % 2
        hi = t_idx // 2
        core_pairs = [(i, i ^ 1) for i in range(n_ten)]
        chip_pairs = [(i, i ^ 2) for i in range(n_ten)]
        states_all = prefix_states[0]
        gain_wide = norm_gain[0].astype(jnp.float32)[None, :]
        sec = lax.axis_index("section")
        n_chunks = 4
        step = rows_local // n_chunks
        outs = []
        previous = None
        for c in range(n_chunks):
            rows = slice(c * step, (c + 1) * step)
            grad_rows_c = grad_cols[:, rows]
            if c > 0:
                grad_rows_c, sent = lax.optimization_barrier((grad_rows_c, sent))
            group_term = lax.dot_general(
                grad_rows_c, weight_local, (((2, 3), (1, 2)), ((), ())),
                preferred_element_type=jnp.float32,
            ).astype(jnp.bfloat16)
            if c == 0:
                key_home, value_home, group_term = lax.optimization_barrier(
                    (key_home, value_home, group_term)
                )
            term4 = group_term.reshape(2, 2, step, width)
            keep = lax.dynamic_index_in_dim(term4, core, 1, False)
            give = lax.dynamic_index_in_dim(term4, 1 - core, 1, False)
            got1 = lax.ppermute(give, "tensor", core_pairs)
            partial = keep.astype(jnp.float32) + got1.astype(jnp.float32)
            mine = lax.dynamic_index_in_dim(partial, hi, 0, False)
            other = lax.dynamic_index_in_dim(partial, 1 - hi, 0, False).astype(jnp.bfloat16)
            if previous is not None:
                other, previous = lax.optimization_barrier((other, previous))
            sent = other
            got2 = lax.ppermute(other, "tensor", chip_pairs)
            normed_grad = mine + got2.astype(jnp.float32)

            states = states_all[rows].astype(jnp.float32)
            inv_rms = lax.rsqrt(jnp.mean(states * states, axis=1, keepdims=True) + EPSILON)
            gained = gain_wide * normed_grad
            layer_term = inv_rms * gained - states * inv_rms**3 * jnp.mean(
                states * gained, axis=1, keepdims=True
            )
            term_low = layer_term.astype(jnp.bfloat16)
            previous = term_low
            if n_sec == 4:
                down = lax.ppermute(term_low, "section", [(3, 2), (2, 1)])
                wrap = lax.ppermute(term_low, "section", [(3, 0)])
                carry = (
                    jnp.where(sec == 1, layer_term, 0.0)
                    + down.astype(jnp.float32)
                    + wrap.astype(jnp.float32)
                )
                last = lax.ppermute(carry.astype(jnp.bfloat16), "section", [(1, 0), (0, 1)])
                outs.append(
                    layer_term
                    + down.astype(jnp.float32)
                    + wrap.astype(jnp.float32)
                    + last.astype(jnp.float32)
                )
            else:
                terms = lax.all_gather(term_low, "section")
                above = jnp.arange(n_sec) > sec
                outs.append(
                    layer_term
                    + jnp.sum(jnp.where(above[:, None, None], terms.astype(jnp.float32), 0.0), axis=0)
                )
        prefix_state_gradient = jnp.concatenate(outs, axis=0)
        return (
            query_grad[None],
            rollout_key_gradient[None],
            suffix_value_grad[None],
            key_home[None],
            value_home[None],
            prefix_state_gradient[None],
        )

    return on_device


def solution(mesh):
    placed = (
        P("section", "sample", "tensor"),
        P("section", "sample", "tensor"),
        P("section", "sample", "tensor"),
        P("section", "sample", "tensor"),
        P("section", ("sample", "tensor"), None),
        P("section", ("sample", "tensor"), None),
        P("section", None, None, "tensor"),
        P("section", ("sample", "tensor"), None),
        P("section", None),
        P("sample", None),
        P("sample", None),
        P(),
    )
    body = make_body(mesh.shape["section"], mesh.shape["sample"], mesh.shape["tensor"])
    return jax.shard_map(
        body,
        mesh=mesh,
        in_specs=placed,
        out_specs=(
            P("section", "sample", "tensor"),
            P("section", "sample", "tensor"),
            P("section", "sample", "tensor"),
            P("section", ("sample", "tensor"), None),
            P("section", ("sample", "tensor"), None),
            P("section", ("sample", "tensor"), None),
        ),
        check_vma=False,
    )
```

```python
import jax
import jax.numpy as jnp
from jax import lax
from jax.sharding import PartitionSpec as P

HEAD_SIZE = 128
PAGE = 128


MASKED_SCORE = -1e30
EPSILON = 1e-05


def visible_keys(seg_row, prompt_row, table, pooled_rows):
    tok_count = seg_row.shape[0]
    seg_hot = seg_row[:, None] == jnp.arange(prompt_row.shape[0], dtype=jnp.int32)[None, :]
    prompt_tok = jnp.sum(jnp.where(seg_hot, prompt_row[None, :], 0), axis=1)
    page_ids = jnp.arange(pooled_rows // PAGE, dtype=jnp.int32)
    member = jnp.any(table[:, :, None] == page_ids[None, None, :], axis=1)
    prompt_hot = prompt_tok[:, None] == jnp.arange(table.shape[0], dtype=jnp.int32)[None, :]
    member_tok = jnp.any(prompt_hot[:, :, None] & member[None, :, :], axis=1)
    prefix_seen = jnp.repeat(member_tok, PAGE, axis=1)
    position = jnp.arange(tok_count, dtype=jnp.int32)
    suffix_seen = (seg_row[:, None] == seg_row[None, :]) & (position[None, :] <= position[:, None])
    return jnp.concatenate([prefix_seen, suffix_seen], axis=1)


def attend_group(query_grp, grad_grp, key_rows, value_rows, visible):
    inv_root = query_grp.shape[-1] ** (-0.5)
    scores = (
        jnp.einsum("rgd,kd->rgk", query_grp, key_rows, preferred_element_type=jnp.float32)
        * inv_root
    )
    scores = jnp.where(visible[:, None, :], scores, MASKED_SCORE)
    row_max = jnp.max(scores, axis=2, keepdims=True)
    exponent = jnp.exp(scores - row_max)
    softmax_w = exponent / jnp.sum(exponent, axis=2, keepdims=True)
    weights_low = softmax_w.astype(jnp.bfloat16)
    attended = jnp.einsum(
        "rgk,kd->rgd", weights_low, value_rows, preferred_element_type=jnp.float32
    )
    delta_row = jnp.sum(grad_grp.astype(jnp.float32) * attended, axis=2, keepdims=True)
    weight_grad = jnp.einsum(
        "rgd,kd->rgk", grad_grp, value_rows, preferred_element_type=jnp.float32
    )
    score_grad = (softmax_w * (weight_grad - delta_row)).astype(jnp.bfloat16)
    key_result = (
        jnp.einsum("rgk,rgd->kd", score_grad, query_grp, preferred_element_type=jnp.float32)
        * inv_root
    )
    value_out = jnp.einsum("rgk,rgd->kd", weights_low, grad_grp, preferred_element_type=jnp.float32)
    return (score_grad, key_result, value_out)


def make_body(n_sec, n_smp, n_ten):
    def on_device(
        queries,
        suffix_keys,
        suffix_values,
        output_grad,
        prefix_keys,
        prefix_values,
        kv_weight,
        prefix_states,
        norm_gain,
        segment_ids,
        segment_prompt,
        block_table,
    ):
        head_width = suffix_keys.shape[2]
        kv_local = head_width // HEAD_SIZE
        rows_local = prefix_keys.shape[1]
        pooled_rows = rows_local * n_smp * n_ten
        block_rows = rows_local * n_ten
        tok_count = queries.shape[1]
        group_size = queries.shape[2] // head_width
        visible = visible_keys(segment_ids[0], segment_prompt[0], block_table, pooled_rows)
        query_rows = queries[0].reshape(tok_count, kv_local, group_size, HEAD_SIZE)
        grad_rows = output_grad[0].reshape(tok_count, kv_local, group_size, HEAD_SIZE)
        own_keys = suffix_keys[0]
        own_values = suffix_values[0]
        pk = prefix_keys[0].reshape(rows_local, n_ten, kv_local, 1, HEAD_SIZE)
        pv = prefix_values[0].reshape(rows_local, n_ten, kv_local, 1, HEAD_SIZE)
        send = jnp.concatenate([pk, pv], axis=3).reshape(rows_local, n_ten, -1).transpose(1, 0, 2)
        got_all = lax.all_to_all(send, "tensor", 0, 0, tiled=True)
        got_all = got_all.reshape(block_rows, kv_local, 2 * HEAD_SIZE)

        query_pieces, suffix_key_pieces, suffix_value_pieces, reduced_pieces = [], [], [], []
        for head_index in range(kv_local):
            low_col = head_index * HEAD_SIZE
            got = got_all[:, head_index]
            if head_index % 2 == 0:
                spread = jnp.broadcast_to(got[None], (n_smp,) + got.shape)
                pool = lax.all_to_all(spread, "sample", 0, 0, tiled=True).reshape(pooled_rows, -1)
            else:
                got, _ = lax.optimization_barrier((got, pool))
                pool = lax.all_gather(got, "sample", axis=0, tiled=True)
            key_rows = jnp.concatenate(
                [pool[:, :HEAD_SIZE], own_keys[:, low_col : low_col + HEAD_SIZE]], axis=0
            )
            value_rows = jnp.concatenate(
                [pool[:, HEAD_SIZE:], own_values[:, low_col : low_col + HEAD_SIZE]], axis=0
            )
            score_grad, key_result, value_out = attend_group(
                query_rows[:, head_index], grad_rows[:, head_index], key_rows, value_rows, visible
            )
            suffix_key_pieces.append(key_result[pooled_rows:])
            suffix_value_pieces.append(value_out[pooled_rows:])
            pool_grad = jnp.concatenate(
                [key_result[:pooled_rows], value_out[:pooled_rows]], axis=1
            ).astype(jnp.bfloat16)
            pool_grad = pool_grad.reshape(n_smp, block_rows, 2 * HEAD_SIZE)
            score_grad, pool_grad = lax.optimization_barrier((score_grad, pool_grad))
            query_pieces.append(
                jnp.einsum("rgk,kd->rgd", score_grad, key_rows, preferred_element_type=jnp.float32)
                * HEAD_SIZE ** (-0.5)
            )
            parts = lax.all_to_all(pool_grad, "sample", 0, 0, tiled=False)
            reduced_pieces.append(jnp.sum(parts.astype(jnp.float32), axis=0))
        query_grad = jnp.stack(query_pieces, axis=1).reshape(tok_count, -1).astype(jnp.bfloat16)
        rollout_key_gradient = jnp.concatenate(suffix_key_pieces, axis=1).astype(jnp.bfloat16)
        suffix_value_grad = jnp.concatenate(suffix_value_pieces, axis=1).astype(jnp.bfloat16)

        reduced = jnp.concatenate(reduced_pieces, axis=1).astype(jnp.bfloat16)
        home_send = reduced.reshape(n_ten, rows_local, kv_local * 2 * HEAD_SIZE)
        home = lax.all_to_all(home_send, "tensor", 0, 0, tiled=True)
        home = home.reshape(n_ten, rows_local, kv_local, 2, HEAD_SIZE).transpose(3, 1, 0, 2, 4)
        home = home.reshape(2, rows_local, n_ten * kv_local * HEAD_SIZE).astype(jnp.float32)
        key_home = home[0]
        value_home = home[1]

        grad_cols = reduced.reshape(block_rows, kv_local, 2, HEAD_SIZE).transpose(0, 2, 1, 3)
        grad_cols = grad_cols.reshape(n_ten, rows_local, 2, kv_local * HEAD_SIZE)
        weight_local = kv_weight[0]
        width = weight_local.shape[0]
        t_idx = lax.axis_index("tensor")
        core = t_idx % 2
        hi = t_idx // 2
        core_pairs = [(i, i ^ 1) for i in range(n_ten)]
        chip_pairs = [(i, i ^ 2) for i in range(n_ten)]
        states_all = prefix_states[0]
        gain_wide = norm_gain[0].astype(jnp.float32)[None, :]
        sec = lax.axis_index("section")
        unit = rows_local // 8
        sizes = [3 * unit, 2 * unit, 2 * unit, unit]
        starts = [sum(sizes[:i]) for i in range(len(sizes))]
        outs = []
        previous = None
        for c in range(len(sizes)):
            step = sizes[c]
            rows = slice(starts[c], starts[c] + step)
            grad_rows_c = grad_cols[:, rows]
            if c > 0:
                grad_rows_c, sent = lax.optimization_barrier((grad_rows_c, sent))
            group_term = lax.dot_general(
                grad_rows_c, weight_local, (((2, 3), (1, 2)), ((), ())),
                preferred_element_type=jnp.float32,
            ).astype(jnp.bfloat16)
            if c == 0:
                key_home, value_home, group_term = lax.optimization_barrier(
                    (key_home, value_home, group_term)
                )
            term4 = group_term.reshape(2, 2, step, width)
            keep = lax.dynamic_index_in_dim(term4, core, 1, False)
            give = lax.dynamic_index_in_dim(term4, 1 - core, 1, False)
            got1 = lax.ppermute(give, "tensor", core_pairs)
            partial = keep.astype(jnp.float32) + got1.astype(jnp.float32)
            mine = lax.dynamic_index_in_dim(partial, hi, 0, False)
            other = lax.dynamic_index_in_dim(partial, 1 - hi, 0, False).astype(jnp.bfloat16)
            if previous is not None:
                other, previous = lax.optimization_barrier((other, previous))
            sent = other
            got2 = lax.ppermute(other, "tensor", chip_pairs)
            normed_grad = mine + got2.astype(jnp.float32)

            states = states_all[rows].astype(jnp.float32)
            inv_rms = lax.rsqrt(jnp.mean(states * states, axis=1, keepdims=True) + EPSILON)
            gained = gain_wide * normed_grad
            layer_term = inv_rms * gained - states * inv_rms**3 * jnp.mean(
                states * gained, axis=1, keepdims=True
            )
            term_low = layer_term.astype(jnp.bfloat16)
            previous = term_low
            if n_sec == 4 and c == len(sizes) - 1:
                total = layer_term
                for shift in range(1, n_sec):
                    pairs = [(l + shift, l) for l in range(n_sec - shift)]
                    total = total + lax.ppermute(term_low, "section", pairs).astype(jnp.float32)
                outs.append(total)
            elif n_sec == 4:
                down = lax.ppermute(term_low, "section", [(3, 2), (2, 1)])
                wrap = lax.ppermute(term_low, "section", [(3, 0)])
                carry = (
                    jnp.where(sec == 1, layer_term, 0.0)
                    + down.astype(jnp.float32)
                    + wrap.astype(jnp.float32)
                )
                last = lax.ppermute(carry.astype(jnp.bfloat16), "section", [(1, 0), (0, 1)])
                outs.append(
                    layer_term
                    + down.astype(jnp.float32)
                    + wrap.astype(jnp.float32)
                    + last.astype(jnp.float32)
                )
            else:
                terms = lax.all_gather(term_low, "section")
                above = jnp.arange(n_sec) > sec
                outs.append(
                    layer_term
                    + jnp.sum(jnp.where(above[:, None, None], terms.astype(jnp.float32), 0.0), axis=0)
                )
        prefix_state_gradient = jnp.concatenate(outs, axis=0)
        return (
            query_grad[None],
            rollout_key_gradient[None],
            suffix_value_grad[None],
            key_home[None],
            value_home[None],
            prefix_state_gradient[None],
        )

    return on_device


def solution(mesh):
    placed = (
        P("section", "sample", "tensor"),
        P("section", "sample", "tensor"),
        P("section", "sample", "tensor"),
        P("section", "sample", "tensor"),
        P("section", ("sample", "tensor"), None),
        P("section", ("sample", "tensor"), None),
        P("section", None, None, "tensor"),
        P("section", ("sample", "tensor"), None),
        P("section", None),
        P("sample", None),
        P("sample", None),
        P(),
    )
    body = make_body(mesh.shape["section"], mesh.shape["sample"], mesh.shape["tensor"])
    return jax.shard_map(
        body,
        mesh=mesh,
        in_specs=placed,
        out_specs=(
            P("section", "sample", "tensor"),
            P("section", "sample", "tensor"),
            P("section", "sample", "tensor"),
            P("section", ("sample", "tensor"), None),
            P("section", ("sample", "tensor"), None),
            P("section", ("sample", "tensor"), None),
        ),
        check_vma=False,
    )
```

```python
import jax
import jax.numpy as jnp
from jax import lax
from jax.sharding import PartitionSpec as P

HEAD_SIZE = 128
PAGE = 128


MASKED_SCORE = -1e30
EPSILON = 1e-05


def visible_keys(seg_row, prompt_row, table, pooled_rows):
    tok_count = seg_row.shape[0]
    seg_hot = seg_row[:, None] == jnp.arange(prompt_row.shape[0], dtype=jnp.int32)[None, :]
    prompt_tok = jnp.sum(jnp.where(seg_hot, prompt_row[None, :], 0), axis=1)
    page_ids = jnp.arange(pooled_rows // PAGE, dtype=jnp.int32)
    member = jnp.any(table[:, :, None] == page_ids[None, None, :], axis=1)
    prompt_hot = prompt_tok[:, None] == jnp.arange(table.shape[0], dtype=jnp.int32)[None, :]
    member_tok = jnp.any(prompt_hot[:, :, None] & member[None, :, :], axis=1)
    prefix_seen = jnp.repeat(member_tok, PAGE, axis=1)
    position = jnp.arange(tok_count, dtype=jnp.int32)
    suffix_seen = (seg_row[:, None] == seg_row[None, :]) & (position[None, :] <= position[:, None])
    return jnp.concatenate([prefix_seen, suffix_seen], axis=1)


def attend_group(query_grp, grad_grp, key_rows, value_rows, visible):
    inv_root = query_grp.shape[-1] ** (-0.5)
    scores = (
        jnp.einsum("rgd,kd->rgk", query_grp, key_rows, preferred_element_type=jnp.float32)
        * inv_root
    )
    scores = jnp.where(visible[:, None, :], scores, MASKED_SCORE)
    row_max = jnp.max(scores, axis=2, keepdims=True)
    exponent = jnp.exp(scores - row_max)
    softmax_w = exponent / jnp.sum(exponent, axis=2, keepdims=True)
    weights_low = softmax_w.astype(jnp.bfloat16)
    attended = jnp.einsum(
        "rgk,kd->rgd", weights_low, value_rows, preferred_element_type=jnp.float32
    )
    delta_row = jnp.sum(grad_grp.astype(jnp.float32) * attended, axis=2, keepdims=True)
    weight_grad = jnp.einsum(
        "rgd,kd->rgk", grad_grp, value_rows, preferred_element_type=jnp.float32
    )
    score_grad = (softmax_w * (weight_grad - delta_row)).astype(jnp.bfloat16)
    key_result = (
        jnp.einsum("rgk,rgd->kd", score_grad, query_grp, preferred_element_type=jnp.float32)
        * inv_root
    )
    value_out = jnp.einsum("rgk,rgd->kd", weights_low, grad_grp, preferred_element_type=jnp.float32)
    return (score_grad, key_result, value_out)


def make_body(n_sec, n_smp, n_ten):
    def on_device(
        queries,
        suffix_keys,
        suffix_values,
        output_grad,
        prefix_keys,
        prefix_values,
        kv_weight,
        prefix_states,
        norm_gain,
        segment_ids,
        segment_prompt,
        block_table,
    ):
        head_width = suffix_keys.shape[2]
        kv_local = head_width // HEAD_SIZE
        rows_local = prefix_keys.shape[1]
        pooled_rows = rows_local * n_smp * n_ten
        block_rows = rows_local * n_ten
        tok_count = queries.shape[1]
        group_size = queries.shape[2] // head_width
        visible = visible_keys(segment_ids[0], segment_prompt[0], block_table, pooled_rows)
        query_rows = queries[0].reshape(tok_count, kv_local, group_size, HEAD_SIZE)
        grad_rows = output_grad[0].reshape(tok_count, kv_local, group_size, HEAD_SIZE)
        own_keys = suffix_keys[0]
        own_values = suffix_values[0]
        pk = prefix_keys[0].reshape(rows_local, n_ten, kv_local, 1, HEAD_SIZE)
        pv = prefix_values[0].reshape(rows_local, n_ten, kv_local, 1, HEAD_SIZE)
        send = jnp.concatenate([pk, pv], axis=3).reshape(rows_local, n_ten, -1).transpose(1, 0, 2)
        got_all = lax.all_to_all(send, "tensor", 0, 0, tiled=True)
        got_all = got_all.reshape(block_rows, kv_local, 2 * HEAD_SIZE)

        query_pieces, suffix_key_pieces, suffix_value_pieces, reduced_pieces = [], [], [], []
        for head_index in range(kv_local):
            low_col = head_index * HEAD_SIZE
            got = got_all[:, head_index]
            if head_index % 2 == 0:
                spread = jnp.broadcast_to(got[None], (n_smp,) + got.shape)
                pool = lax.all_to_all(spread, "sample", 0, 0, tiled=True).reshape(pooled_rows, -1)
            else:
                got, _ = lax.optimization_barrier((got, pool))
                pool = lax.all_gather(got, "sample", axis=0, tiled=True)
            key_rows = jnp.concatenate(
                [pool[:, :HEAD_SIZE], own_keys[:, low_col : low_col + HEAD_SIZE]], axis=0
            )
            value_rows = jnp.concatenate(
                [pool[:, HEAD_SIZE:], own_values[:, low_col : low_col + HEAD_SIZE]], axis=0
            )
            score_grad, key_result, value_out = attend_group(
                query_rows[:, head_index], grad_rows[:, head_index], key_rows, value_rows, visible
            )
            suffix_key_pieces.append(key_result[pooled_rows:])
            suffix_value_pieces.append(value_out[pooled_rows:])
            pool_grad = jnp.concatenate(
                [key_result[:pooled_rows], value_out[:pooled_rows]], axis=1
            ).astype(jnp.bfloat16)
            pool_grad = pool_grad.reshape(n_smp, block_rows, 2 * HEAD_SIZE)
            score_grad, pool_grad = lax.optimization_barrier((score_grad, pool_grad))
            query_pieces.append(
                jnp.einsum("rgk,kd->rgd", score_grad, key_rows, preferred_element_type=jnp.float32)
                * HEAD_SIZE ** (-0.5)
            )
            parts = lax.all_to_all(pool_grad, "sample", 0, 0, tiled=False)
            reduced_pieces.append(jnp.sum(parts.astype(jnp.float32), axis=0))
        query_grad = jnp.stack(query_pieces, axis=1).reshape(tok_count, -1).astype(jnp.bfloat16)
        rollout_key_gradient = jnp.concatenate(suffix_key_pieces, axis=1).astype(jnp.bfloat16)
        suffix_value_grad = jnp.concatenate(suffix_value_pieces, axis=1).astype(jnp.bfloat16)

        reduced = jnp.concatenate(reduced_pieces, axis=1).astype(jnp.bfloat16)
        home_send = reduced.reshape(n_ten, rows_local, kv_local * 2 * HEAD_SIZE)
        home = lax.all_to_all(home_send, "tensor", 0, 0, tiled=True)
        home = home.reshape(n_ten, rows_local, kv_local, 2, HEAD_SIZE).transpose(3, 1, 0, 2, 4)
        home = home.reshape(2, rows_local, n_ten * kv_local * HEAD_SIZE).astype(jnp.float32)
        key_home = home[0]
        value_home = home[1]

        grad_cols = reduced.reshape(block_rows, kv_local, 2, HEAD_SIZE).transpose(0, 2, 1, 3)
        grad_cols = grad_cols.reshape(n_ten, rows_local, 2, kv_local * HEAD_SIZE)
        weight_local = kv_weight[0]
        width = weight_local.shape[0]
        t_idx = lax.axis_index("tensor")
        core = t_idx % 2
        hi = t_idx // 2
        core_pairs = [(i, i ^ 1) for i in range(n_ten)]
        chip_pairs = [(i, i ^ 2) for i in range(n_ten)]
        states_all = prefix_states[0]
        gain_wide = norm_gain[0].astype(jnp.float32)[None, :]
        sec = lax.axis_index("section")
        unit = rows_local // 8
        sizes = [3 * unit, 2 * unit, 2 * unit, unit]
        starts = [sum(sizes[:i]) for i in range(len(sizes))]
        outs = []
        previous = None
        for c in range(len(sizes)):
            step = sizes[c]
            rows = slice(starts[c], starts[c] + step)
            grad_rows_c = grad_cols[:, rows]
            if c > 0:
                grad_rows_c, sent = lax.optimization_barrier((grad_rows_c, sent))
            group_term = lax.dot_general(
                grad_rows_c, weight_local, (((2, 3), (1, 2)), ((), ())),
                preferred_element_type=jnp.float32,
            ).astype(jnp.bfloat16)
            if c == 0:
                key_home, value_home, group_term = lax.optimization_barrier(
                    (key_home, value_home, group_term)
                )
            term4 = group_term.reshape(2, 2, step, width)
            keep = lax.dynamic_index_in_dim(term4, core, 1, False)
            give = lax.dynamic_index_in_dim(term4, 1 - core, 1, False)
            got1 = lax.ppermute(give, "tensor", core_pairs)
            partial = keep.astype(jnp.float32) + got1.astype(jnp.float32)
            mine = lax.dynamic_index_in_dim(partial, hi, 0, False)
            other = lax.dynamic_index_in_dim(partial, 1 - hi, 0, False).astype(jnp.bfloat16)
            if previous is not None:
                other, previous = lax.optimization_barrier((other, previous))
            sent = other
            got2 = lax.ppermute(other, "tensor", chip_pairs)
            normed_grad = mine + got2.astype(jnp.float32)

            states = states_all[rows].astype(jnp.float32)
            inv_rms = lax.rsqrt(jnp.mean(states * states, axis=1, keepdims=True) + EPSILON)
            gained = gain_wide * normed_grad
            layer_term = inv_rms * gained - states * inv_rms**3 * jnp.mean(
                states * gained, axis=1, keepdims=True
            )
            term_low = layer_term.astype(jnp.bfloat16)
            previous = term_low
            if n_sec == 4 and c >= len(sizes) - 2:
                total = layer_term
                for shift in range(1, n_sec):
                    pairs = [(l + shift, l) for l in range(n_sec - shift)]
                    total = total + lax.ppermute(term_low, "section", pairs).astype(jnp.float32)
                outs.append(total)
            elif n_sec == 4:
                down = lax.ppermute(term_low, "section", [(3, 2), (2, 1)])
                wrap = lax.ppermute(term_low, "section", [(3, 0)])
                carry = (
                    jnp.where(sec == 1, layer_term, 0.0)
                    + down.astype(jnp.float32)
                    + wrap.astype(jnp.float32)
                )
                last = lax.ppermute(carry.astype(jnp.bfloat16), "section", [(1, 0), (0, 1)])
                outs.append(
                    layer_term
                    + down.astype(jnp.float32)
                    + wrap.astype(jnp.float32)
                    + last.astype(jnp.float32)
                )
            else:
                terms = lax.all_gather(term_low, "section")
                above = jnp.arange(n_sec) > sec
                outs.append(
                    layer_term
                    + jnp.sum(jnp.where(above[:, None, None], terms.astype(jnp.float32), 0.0), axis=0)
                )
        prefix_state_gradient = jnp.concatenate(outs, axis=0)
        return (
            query_grad[None],
            rollout_key_gradient[None],
            suffix_value_grad[None],
            key_home[None],
            value_home[None],
            prefix_state_gradient[None],
        )

    return on_device


def solution(mesh):
    placed = (
        P("section", "sample", "tensor"),
        P("section", "sample", "tensor"),
        P("section", "sample", "tensor"),
        P("section", "sample", "tensor"),
        P("section", ("sample", "tensor"), None),
        P("section", ("sample", "tensor"), None),
        P("section", None, None, "tensor"),
        P("section", ("sample", "tensor"), None),
        P("section", None),
        P("sample", None),
        P("sample", None),
        P(),
    )
    body = make_body(mesh.shape["section"], mesh.shape["sample"], mesh.shape["tensor"])
    return jax.shard_map(
        body,
        mesh=mesh,
        in_specs=placed,
        out_specs=(
            P("section", "sample", "tensor"),
            P("section", "sample", "tensor"),
            P("section", "sample", "tensor"),
            P("section", ("sample", "tensor"), None),
            P("section", ("sample", "tensor"), None),
            P("section", ("sample", "tensor"), None),
        ),
        check_vma=False,
    )
```

```python
import jax
import jax.numpy as jnp
from jax import lax
from jax.sharding import PartitionSpec as P

HEAD_SIZE = 128
PAGE = 128


MASKED_SCORE = -1e30
EPSILON = 1e-05


def visible_keys(seg_row, prompt_row, table, pooled_rows):
    tok_count = seg_row.shape[0]
    seg_hot = seg_row[:, None] == jnp.arange(prompt_row.shape[0], dtype=jnp.int32)[None, :]
    prompt_tok = jnp.sum(jnp.where(seg_hot, prompt_row[None, :], 0), axis=1)
    page_ids = jnp.arange(pooled_rows // PAGE, dtype=jnp.int32)
    member = jnp.any(table[:, :, None] == page_ids[None, None, :], axis=1)
    prompt_hot = prompt_tok[:, None] == jnp.arange(table.shape[0], dtype=jnp.int32)[None, :]
    member_tok = jnp.any(prompt_hot[:, :, None] & member[None, :, :], axis=1)
    prefix_seen = jnp.repeat(member_tok, PAGE, axis=1)
    position = jnp.arange(tok_count, dtype=jnp.int32)
    suffix_seen = (seg_row[:, None] == seg_row[None, :]) & (position[None, :] <= position[:, None])
    return jnp.concatenate([prefix_seen, suffix_seen], axis=1)


def attend_group(query_grp, grad_grp, key_rows, value_rows, visible):
    inv_root = query_grp.shape[-1] ** (-0.5)
    scores = (
        jnp.einsum("rgd,kd->rgk", query_grp, key_rows, preferred_element_type=jnp.float32)
        * inv_root
    )
    scores = jnp.where(visible[:, None, :], scores, MASKED_SCORE)
    row_max = jnp.max(scores, axis=2, keepdims=True)
    exponent = jnp.exp(scores - row_max)
    softmax_w = exponent / jnp.sum(exponent, axis=2, keepdims=True)
    weights_low = softmax_w.astype(jnp.bfloat16)
    attended = jnp.einsum(
        "rgk,kd->rgd", weights_low, value_rows, preferred_element_type=jnp.float32
    )
    delta_row = jnp.sum(grad_grp.astype(jnp.float32) * attended, axis=2, keepdims=True)
    weight_grad = jnp.einsum(
        "rgd,kd->rgk", grad_grp, value_rows, preferred_element_type=jnp.float32
    )
    score_grad = (softmax_w * (weight_grad - delta_row)).astype(jnp.bfloat16)
    key_result = (
        jnp.einsum("rgk,rgd->kd", score_grad, query_grp, preferred_element_type=jnp.float32)
        * inv_root
    )
    value_out = jnp.einsum("rgk,rgd->kd", weights_low, grad_grp, preferred_element_type=jnp.float32)
    return (score_grad, key_result, value_out)


def make_body(n_sec, n_smp, n_ten):
    def on_device(
        queries,
        suffix_keys,
        suffix_values,
        output_grad,
        prefix_keys,
        prefix_values,
        kv_weight,
        prefix_states,
        norm_gain,
        segment_ids,
        segment_prompt,
        block_table,
    ):
        head_width = suffix_keys.shape[2]
        kv_local = head_width // HEAD_SIZE
        rows_local = prefix_keys.shape[1]
        pooled_rows = rows_local * n_smp * n_ten
        block_rows = rows_local * n_ten
        tok_count = queries.shape[1]
        group_size = queries.shape[2] // head_width
        visible = visible_keys(segment_ids[0], segment_prompt[0], block_table, pooled_rows)
        query_rows = queries[0].reshape(tok_count, kv_local, group_size, HEAD_SIZE)
        grad_rows = output_grad[0].reshape(tok_count, kv_local, group_size, HEAD_SIZE)
        own_keys = suffix_keys[0]
        own_values = suffix_values[0]
        pk = prefix_keys[0].reshape(rows_local, n_ten, kv_local, 1, HEAD_SIZE)
        pv = prefix_values[0].reshape(rows_local, n_ten, kv_local, 1, HEAD_SIZE)
        send = jnp.concatenate([pk, pv], axis=3).reshape(rows_local, n_ten, -1).transpose(1, 0, 2)
        got_all = lax.all_to_all(send, "tensor", 0, 0, tiled=True)
        got_all = got_all.reshape(block_rows, kv_local, 2 * HEAD_SIZE)

        query_pieces, suffix_key_pieces, suffix_value_pieces, reduced_pieces = [], [], [], []
        for head_index in range(kv_local):
            low_col = head_index * HEAD_SIZE
            got = got_all[:, head_index]
            if head_index % 2 == 0:
                spread = jnp.broadcast_to(got[None], (n_smp,) + got.shape)
                pool = lax.all_to_all(spread, "sample", 0, 0, tiled=True).reshape(pooled_rows, -1)
            else:
                got, _ = lax.optimization_barrier((got, pool))
                pool = lax.all_gather(got, "sample", axis=0, tiled=True)
            key_rows = jnp.concatenate(
                [pool[:, :HEAD_SIZE], own_keys[:, low_col : low_col + HEAD_SIZE]], axis=0
            )
            value_rows = jnp.concatenate(
                [pool[:, HEAD_SIZE:], own_values[:, low_col : low_col + HEAD_SIZE]], axis=0
            )
            score_grad, key_result, value_out = attend_group(
                query_rows[:, head_index], grad_rows[:, head_index], key_rows, value_rows, visible
            )
            suffix_key_pieces.append(key_result[pooled_rows:])
            suffix_value_pieces.append(value_out[pooled_rows:])
            pool_grad = jnp.concatenate(
                [key_result[:pooled_rows], value_out[:pooled_rows]], axis=1
            ).astype(jnp.bfloat16)
            pool_grad = pool_grad.reshape(n_smp, block_rows, 2 * HEAD_SIZE)
            score_grad, pool_grad = lax.optimization_barrier((score_grad, pool_grad))
            query_pieces.append(
                jnp.einsum("rgk,kd->rgd", score_grad, key_rows, preferred_element_type=jnp.float32)
                * HEAD_SIZE ** (-0.5)
            )
            parts = lax.all_to_all(pool_grad, "sample", 0, 0, tiled=False)
            reduced_pieces.append(jnp.sum(parts.astype(jnp.float32), axis=0))
        query_grad = jnp.stack(query_pieces, axis=1).reshape(tok_count, -1).astype(jnp.bfloat16)
        rollout_key_gradient = jnp.concatenate(suffix_key_pieces, axis=1).astype(jnp.bfloat16)
        suffix_value_grad = jnp.concatenate(suffix_value_pieces, axis=1).astype(jnp.bfloat16)

        reduced = jnp.concatenate(reduced_pieces, axis=1).astype(jnp.bfloat16)
        home_send = reduced.reshape(n_ten, rows_local, kv_local * 2 * HEAD_SIZE)
        home = lax.all_to_all(home_send, "tensor", 0, 0, tiled=True)
        home = home.reshape(n_ten, rows_local, kv_local, 2, HEAD_SIZE).transpose(3, 1, 0, 2, 4)
        home = home.reshape(2, rows_local, n_ten * kv_local * HEAD_SIZE).astype(jnp.float32)
        key_home = home[0]
        value_home = home[1]

        grad_cols = reduced.reshape(block_rows, kv_local, 2, HEAD_SIZE).transpose(0, 2, 1, 3)
        grad_cols = grad_cols.reshape(n_ten, rows_local, 2, kv_local * HEAD_SIZE)
        weight_local = kv_weight[0]
        width = weight_local.shape[0]
        t_idx = lax.axis_index("tensor")
        core = t_idx % 2
        hi = t_idx // 2
        core_pairs = [(i, i ^ 1) for i in range(n_ten)]
        chip_pairs = [(i, i ^ 2) for i in range(n_ten)]
        states_all = prefix_states[0]
        gain_wide = norm_gain[0].astype(jnp.float32)[None, :]
        sec = lax.axis_index("section")
        unit = rows_local // 8
        sizes = [4 * unit, 2 * unit, unit, unit]
        starts = [sum(sizes[:i]) for i in range(len(sizes))]
        outs = []
        previous = None
        for c in range(len(sizes)):
            step = sizes[c]
            rows = slice(starts[c], starts[c] + step)
            grad_rows_c = grad_cols[:, rows]
            if c > 0:
                grad_rows_c, sent = lax.optimization_barrier((grad_rows_c, sent))
            group_term = lax.dot_general(
                grad_rows_c, weight_local, (((2, 3), (1, 2)), ((), ())),
                preferred_element_type=jnp.float32,
            ).astype(jnp.bfloat16)
            if c == 0:
                key_home, value_home, group_term = lax.optimization_barrier(
                    (key_home, value_home, group_term)
                )
            term4 = group_term.reshape(2, 2, step, width)
            keep = lax.dynamic_index_in_dim(term4, core, 1, False)
            give = lax.dynamic_index_in_dim(term4, 1 - core, 1, False)
            got1 = lax.ppermute(give, "tensor", core_pairs)
            partial = keep.astype(jnp.float32) + got1.astype(jnp.float32)
            mine = lax.dynamic_index_in_dim(partial, hi, 0, False)
            other = lax.dynamic_index_in_dim(partial, 1 - hi, 0, False).astype(jnp.bfloat16)
            if previous is not None:
                other, previous = lax.optimization_barrier((other, previous))
            sent = other
            got2 = lax.ppermute(other, "tensor", chip_pairs)
            normed_grad = mine + got2.astype(jnp.float32)

            states = states_all[rows].astype(jnp.float32)
            inv_rms = lax.rsqrt(jnp.mean(states * states, axis=1, keepdims=True) + EPSILON)
            gained = gain_wide * normed_grad
            layer_term = inv_rms * gained - states * inv_rms**3 * jnp.mean(
                states * gained, axis=1, keepdims=True
            )
            term_low = layer_term.astype(jnp.bfloat16)
            previous = term_low
            if n_sec == 4 and c == len(sizes) - 1:
                total = layer_term
                for shift in range(1, n_sec):
                    pairs = [(l + shift, l) for l in range(n_sec - shift)]
                    total = total + lax.ppermute(term_low, "section", pairs).astype(jnp.float32)
                outs.append(total)
            elif n_sec == 4:
                down = lax.ppermute(term_low, "section", [(3, 2), (2, 1)])
                wrap = lax.ppermute(term_low, "section", [(3, 0)])
                carry = (
                    jnp.where(sec == 1, layer_term, 0.0)
                    + down.astype(jnp.float32)
                    + wrap.astype(jnp.float32)
                )
                last = lax.ppermute(carry.astype(jnp.bfloat16), "section", [(1, 0), (0, 1)])
                outs.append(
                    layer_term
                    + down.astype(jnp.float32)
                    + wrap.astype(jnp.float32)
                    + last.astype(jnp.float32)
                )
            else:
                terms = lax.all_gather(term_low, "section")
                above = jnp.arange(n_sec) > sec
                outs.append(
                    layer_term
                    + jnp.sum(jnp.where(above[:, None, None], terms.astype(jnp.float32), 0.0), axis=0)
                )
        prefix_state_gradient = jnp.concatenate(outs, axis=0)
        return (
            query_grad[None],
            rollout_key_gradient[None],
            suffix_value_grad[None],
            key_home[None],
            value_home[None],
            prefix_state_gradient[None],
        )

    return on_device


def solution(mesh):
    placed = (
        P("section", "sample", "tensor"),
        P("section", "sample", "tensor"),
        P("section", "sample", "tensor"),
        P("section", "sample", "tensor"),
        P("section", ("sample", "tensor"), None),
        P("section", ("sample", "tensor"), None),
        P("section", None, None, "tensor"),
        P("section", ("sample", "tensor"), None),
        P("section", None),
        P("sample", None),
        P("sample", None),
        P(),
    )
    body = make_body(mesh.shape["section"], mesh.shape["sample"], mesh.shape["tensor"])
    return jax.shard_map(
        body,
        mesh=mesh,
        in_specs=placed,
        out_specs=(
            P("section", "sample", "tensor"),
            P("section", "sample", "tensor"),
            P("section", "sample", "tensor"),
            P("section", ("sample", "tensor"), None),
            P("section", ("sample", "tensor"), None),
            P("section", ("sample", "tensor"), None),
        ),
        check_vma=False,
    )
```
